256 devices in a mesh: rows: 64 (over z, y, core), cols: 4 (over x).
Axes of the slice: x: 4, y: 4, z: 8, core: 2. Of those that a mesh axis runs over, the one named last changes fastest.
Arguments:
- images: bfloat16 [512, 360, 128], P('rows'), may hold values from -8 to 8
- partners: int32 [64, 8], P('rows'), may hold values from 0 to 7, each once within a row
- counts: int32 [64], P('rows'), may hold values from 1 to 8
- start: float32 [64, 24], P('rows'), may hold values from -6 to 6
Outputs:
- first_vec: float32 [64, 24], P('rows')
- second_vec: float32 [64, 24], P('rows')
The draws below stay inside these ranges and needn't reach their ends.
Inputs may be any that keep to these rules, and one draw needn't show every extreme that they name: Each row of partners lists every code of 0 to 7 once; only its first counts[I] entries are pairs.
All inputs are finite; a program needn't handle non-finite values.
Results may differ from the reference program's by a relative error of at most 0.0003.
Values may be sent and summed in bfloat16 or wider, within the bound.
No kernel may reach another device: no remote copies, remote signals or barrier semaphores. Data moves between devices by JAX's collectives and lax.ppermute only.
A program may use at most 64 MiB of HBM per device.

```python
import math
import jax
import jax.numpy as jnp
from jax import lax

LINES = 360
RADII = 128
IMG_BLK = 8
NBLK = 64
SLOTS = 8
HALO = 4
IMAGES = 512
VEC = 24


def draw_images(key, part):
    key_noise = jax.random.fold_in(key, 0)
    noise = jax.random.normal(key_noise, (IMAGES, LINES, RADII), jnp.float32)
    values = noise
    return jnp.clip(values, -8.0, 8.0).astype(jnp.bfloat16)


def draw_start(key, part):
    key_values = jax.random.fold_in(key, 0)
    values = jnp.clip(jax.random.normal(key_values, (NBLK, VEC), jnp.float32), -6.0, 6.0)
    return values.astype(jnp.float32)


def plant(array, rng, low, high):
    longest = array.shape.index(max(array.shape))
    spots = []
    for shift in (0, 1):
        where = [jax.random.randint(jax.random.fold_in(rng, axis), (), 0, length) for axis, length in enumerate(array.shape)]
        where[longest] = (where[longest] + shift) % array.shape[longest]
        spots.append(tuple(where))
    return array.at[spots[0]].set(low).at[spots[1]].set(high)


def setup_inputs(seed: int = 0) -> dict:
    arg_keys = jax.random.split(jax.random.key(seed), 5)
    return {
        "images": draw_images(jax.random.fold_in(arg_keys[4], 71), 0),
        "partners": jax.vmap(lambda own: jax.random.permutation(own, SLOTS))(jax.random.split(arg_keys[1], NBLK)).reshape((NBLK, SLOTS)).astype(jnp.int32),
        "counts": plant(jax.random.randint(arg_keys[2], (NBLK,), 1, SLOTS + 1), jax.random.fold_in(arg_keys[2], 1), 1, SLOTS).astype(jnp.int32),
        "start": draw_start(jax.random.fold_in(arg_keys[4], 71), 0),
    }


score_gain = 0.4
norm_eps = 1e-06

def line_table(lines):
    angle = 2.0 * math.pi * jnp.arange(lines).astype(jnp.float32) / lines
    return jnp.stack([jnp.cos(angle), jnp.sin(angle), jnp.cos(2.0 * angle)], axis=1)

def pair_tile(own, other, table):
    count, lines, radii = own.shape
    others = other.shape[0]
    flat = other.reshape(others * lines, radii)

    def one_image(lines_a):
        scores = lax.dot_general(lines_a, flat, (((1,), (1,)), ((), ())), preferred_element_type=jnp.float32) * score_gain
        shaped = scores.reshape(lines, others, lines)
        top = lax.optimization_barrier(jnp.max(shaped, axis=(0, 2)))
        weights = jnp.exp(shaped - top[None, :, None])
        total = lax.optimization_barrier(jnp.sum(weights, axis=(0, 2)))
        left = jnp.einsum('lp,lbk->pbk', table, weights, precision=lax.Precision.HIGHEST)
        rel = jnp.einsum('pbk,kq->pbq', left, table, precision=lax.Precision.HIGHEST)
        return rel / total[None, :, None]
    stacked = lax.map(one_image, own)
    return jnp.transpose(stacked, (1, 0, 3, 2)).reshape(3 * count, 3 * others)

def offsets_of(codes, halo):
    return jnp.where(codes < halo, codes - halo, codes - halo + 1).astype(jnp.int32)

def reference(images, partners, counts, start):
    blocks = images.reshape(NBLK, IMG_BLK, LINES, RADII)
    table = line_table(LINES)
    block_ids = jnp.arange(NBLK).astype(jnp.int32)
    partner_ids = (block_ids[:, None] + offsets_of(partners, HALO)) % NBLK
    valid = jnp.arange(SLOTS).astype(jnp.int32)[None, :] < counts[:, None]

    def row_tiles(index):
        own = lax.dynamic_index_in_dim(blocks, index, 0, keepdims=False)

        def slot_tile(slot):
            other = lax.dynamic_index_in_dim(blocks, partner_ids[index, slot], 0, keepdims=False)
            return lax.cond(slot < counts[index], lambda: pair_tile(own, other, table), lambda: jnp.zeros((VEC, VEC), jnp.float32))
        return lax.map(slot_tile, jnp.arange(SLOTS).astype(jnp.int32))
    tiles = lax.map(row_tiles, block_ids)

    def apply(vector):
        picked = vector[partner_ids]
        products = jnp.einsum('nsvw,nsw->nsv', tiles, picked, precision=lax.Precision.HIGHEST)
        return lax.optimization_barrier(jnp.sum(jnp.where(valid[:, :, None], products, 0.0), axis=1))
    first_raw = apply(start)
    first_vec = first_raw / jnp.sqrt(jnp.mean(first_raw * first_raw) + norm_eps)
    second_raw = apply(first_vec)
    second_vec = second_raw / jnp.sqrt(jnp.mean(second_raw * second_raw) + norm_eps)
    return (first_vec, second_vec)
```

```python
import math

import jax
import jax.numpy as jnp
from jax import lax
from jax.experimental import pallas as pl
from jax.experimental.pallas import tpu as pltpu
from jax.sharding import PartitionSpec as P

score_gain = 0.4
norm_eps = 1e-06
HIGH = lax.Precision.HIGHEST


def line_table(lines):
    angle = 2.0 * math.pi * jnp.arange(lines).astype(jnp.float32) / lines
    return jnp.stack([jnp.cos(angle), jnp.sin(angle), jnp.cos(2.0 * angle)], axis=1)


def tile_kernel(a_ref, b_ref, w_ref, o_ref):
    n = a_ref.shape[0]

    def body(i, carry):
        a = i // n
        b = i % n
        s = lax.dot_general(
            b_ref[b], a_ref[a], (((1,), (1,)), ((), ())), preferred_element_type=jnp.float32
        )
        s = s * score_gain
        top = jnp.max(s, axis=0, keepdims=True)
        e = jnp.exp(s - top)
        o_ref[a, b, 0:1, :] = top
        o_ref[a, b, 1:2, :] = jnp.sum(e, axis=0, keepdims=True)
        o_ref[a, b, 2:3, :] = jnp.sum(e * w_ref[0], axis=0, keepdims=True)
        o_ref[a, b, 3:4, :] = jnp.sum(e * w_ref[1], axis=0, keepdims=True)
        o_ref[a, b, 4:5, :] = jnp.sum(e * w_ref[2], axis=0, keepdims=True)
        return carry

    lax.fori_loop(0, n * n, body, 0)


def pair_tile(own, other, table):
    count, lines, radii = own.shape
    padded = ((lines + 127) // 128) * 128
    own_p = jnp.pad(own, ((0, 0), (0, padded - lines), (0, 0)))
    wide = jnp.broadcast_to(jnp.transpose(table)[:, :, None], (3, lines, padded))
    stats = pl.pallas_call(
        tile_kernel,
        out_shape=jax.ShapeDtypeStruct((count, count, 8, padded), jnp.float32),
        in_specs=[pl.BlockSpec(memory_space=pltpu.VMEM)] * 3,
        out_specs=pl.BlockSpec(memory_space=pltpu.VMEM),
        compiler_params=pltpu.CompilerParams(vmem_limit_bytes=48 * 1024 * 1024),
    )(own_p, other, wide)
    stats = stats[:, :, :, :lines]
    top = stats[:, :, 0, :]
    peak = jnp.max(top, axis=2, keepdims=True)
    scale = jnp.exp(top - peak)
    total = jnp.sum(scale * stats[:, :, 1, :], axis=2)
    sums = stats[:, :, 2:5, :] * scale[:, :, None, :]
    rel = jnp.einsum("lp,abql->abpq", table, sums, precision=HIGH)
    rel = rel / total[:, :, None, None]
    return jnp.transpose(rel, (2, 0, 3, 1)).reshape(3 * count, 3 * count)


def body(images, partners, counts, start):
    count, lines, radii = images.shape
    width = 3 * count
    slots = partners.shape[1]
    halo = slots // 2
    ncols = lax.axis_size("cols")
    nblk = lax.axis_size("rows")
    row = lax.axis_index("rows")
    column = lax.axis_index("cols")
    step = column + 1
    table = line_table(lines)

    axes = ("rows", "cols")
    route = []
    for i in range(nblk):
        for c in range(ncols):
            route.append((((i + c + 1) % nblk) * ncols + c, i * ncols + c))
    fetch = lambda v: lax.ppermute(v, axes, route)
    other = fetch(images)
    other_partners = fetch(partners)
    other_counts = fetch(counts)
    other_start = fetch(start)

    tile = pair_tile(images, other, table)

    slot_ids = jnp.arange(slots)
    plus = jnp.any((partners[0] == step + halo - 1) & (slot_ids < counts[0]))
    minus = jnp.any((other_partners[0] == halo - step) & (slot_ids < other_counts[0]))
    partner_row = (row + step) % nblk
    rows_ids = jnp.arange(nblk)
    at_own = (rows_ids == row)[:, None]
    at_other = (rows_ids == partner_row)[:, None]

    def spread(x_own, x_other):
        forward = jnp.where(plus, jnp.dot(tile, x_other, precision=HIGH), 0.0)
        backward = jnp.where(minus, jnp.dot(tile.T, x_own, precision=HIGH), 0.0)
        part = jnp.where(at_own, forward[None, :], 0.0) + jnp.where(at_other, backward[None, :], 0.0)
        return lax.psum(part, axes)

    entries = float(width * nblk)

    def normalize(raw):
        return raw / jnp.sqrt(jnp.sum(raw * raw) / entries + norm_eps)

    first_all = normalize(spread(start[0], other_start[0]))
    first_own = lax.dynamic_index_in_dim(first_all, row, 0, keepdims=True)
    first_other = lax.dynamic_index_in_dim(first_all, partner_row, 0, keepdims=False)
    second_all = normalize(spread(first_own[0], first_other))
    second_own = lax.dynamic_index_in_dim(second_all, row, 0, keepdims=True)
    return (first_own, second_own)


def solution(mesh):
    in_specs = (P("rows", None, None), P("rows", None), P("rows"), P("rows", None))
    out_specs = (P("rows", None), P("rows", None))
    return jax.shard_map(body, mesh=mesh, in_specs=in_specs, out_specs=out_specs, check_vma=False)
```

```python
import math

import jax
import jax.numpy as jnp
from jax import lax
from jax.experimental import pallas as pl
from jax.experimental.pallas import tpu as pltpu
from jax.sharding import PartitionSpec as P

score_gain = 0.4
norm_eps = 1e-06
HIGH = lax.Precision.HIGHEST


def line_table(lines):
    angle = 2.0 * math.pi * jnp.arange(lines).astype(jnp.float32) / lines
    return jnp.stack([jnp.cos(angle), jnp.sin(angle), jnp.cos(2.0 * angle)], axis=1)


def tile_kernel(a_ref, b_ref, w_ref, o_ref):
    n = a_ref.shape[0]

    def body(i, carry):
        a = i // n
        b = i % n
        s = lax.dot_general(
            b_ref[b], a_ref[a], (((1,), (1,)), ((), ())), preferred_element_type=jnp.float32
        )
        s = s * score_gain
        top = jnp.max(s, axis=0, keepdims=True)
        e = jnp.exp(s - top)
        o_ref[a, b, 0:1, :] = top
        o_ref[a, b, 1:2, :] = jnp.sum(e, axis=0, keepdims=True)
        o_ref[a, b, 2:3, :] = jnp.sum(e * w_ref[0], axis=0, keepdims=True)
        o_ref[a, b, 3:4, :] = jnp.sum(e * w_ref[1], axis=0, keepdims=True)
        o_ref[a, b, 4:5, :] = jnp.sum(e * w_ref[2], axis=0, keepdims=True)
        return carry

    lax.fori_loop(0, n * n, body, 0)


def pair_tile(own, other, table):
    count, lines, radii = own.shape
    padded = ((lines + 127) // 128) * 128
    own_p = jnp.pad(own, ((0, 0), (0, padded - lines), (0, 0)))
    wide = jnp.broadcast_to(jnp.transpose(table)[:, :, None], (3, lines, padded))
    stats = pl.pallas_call(
        tile_kernel,
        out_shape=jax.ShapeDtypeStruct((count, count, 8, padded), jnp.float32),
        in_specs=[pl.BlockSpec(memory_space=pltpu.VMEM)] * 3,
        out_specs=pl.BlockSpec(memory_space=pltpu.VMEM),
        compiler_params=pltpu.CompilerParams(vmem_limit_bytes=48 * 1024 * 1024),
    )(own_p, other, wide)
    stats = stats[:, :, :, :lines]
    top = stats[:, :, 0, :]
    peak = jnp.max(top, axis=2, keepdims=True)
    scale = jnp.exp(top - peak)
    total = jnp.sum(scale * stats[:, :, 1, :], axis=2)
    sums = stats[:, :, 2:5, :] * scale[:, :, None, :]
    rel = jnp.einsum("lp,abql->abpq", table, sums, precision=HIGH)
    rel = rel / total[:, :, None, None]
    return jnp.transpose(rel, (2, 0, 3, 1)).reshape(3 * count, 3 * count)


def butterfly_sum(value, axes, size):
    bit = 1
    while bit < size:
        route = [(i, i ^ bit) for i in range(size)]
        value = value + lax.ppermute(value, axes, route)
        bit *= 2
    return value


def body(images, partners, counts, start):
    count, lines, radii = images.shape
    width = 3 * count
    slots = partners.shape[1]
    halo = slots // 2
    ncols = lax.axis_size("cols")
    nblk = lax.axis_size("rows")
    row = lax.axis_index("rows")
    column = lax.axis_index("cols")
    step = column + 1
    table = line_table(lines)

    axes = ("rows", "cols")
    route = []
    for i in range(nblk):
        for c in range(ncols):
            route.append((((i + c + 1) % nblk) * ncols + c, i * ncols + c))
    fetch = lambda v: lax.ppermute(v, axes, route)
    other = fetch(images)
    other_partners = fetch(partners)
    other_counts = fetch(counts)
    other_start = fetch(start)

    tile = pair_tile(images, other, table)

    slot_ids = jnp.arange(slots)
    plus = jnp.any((partners[0] == step + halo - 1) & (slot_ids < counts[0]))
    minus = jnp.any((other_partners[0] == halo - step) & (slot_ids < other_counts[0]))
    partner_row = (row + step) % nblk
    rows_ids = jnp.arange(nblk)
    at_own = (rows_ids == row)[:, None]
    at_other = (rows_ids == partner_row)[:, None]

    def spread(x_own, x_other):
        forward = jnp.where(plus, jnp.dot(tile, x_other, precision=HIGH), 0.0)
        backward = jnp.where(minus, jnp.dot(tile.T, x_own, precision=HIGH), 0.0)
        part = jnp.where(at_own, forward[None, :], 0.0) + jnp.where(at_other, backward[None, :], 0.0)
        return butterfly_sum(part, axes, nblk * ncols)

    entries = float(width * nblk)

    def normalize(raw):
        return raw / jnp.sqrt(jnp.sum(raw * raw) / entries + norm_eps)

    first_all = normalize(spread(start[0], other_start[0]))
    first_own = lax.dynamic_index_in_dim(first_all, row, 0, keepdims=True)
    first_other = lax.dynamic_index_in_dim(first_all, partner_row, 0, keepdims=False)
    second_all = normalize(spread(first_own[0], first_other))
    second_own = lax.dynamic_index_in_dim(second_all, row, 0, keepdims=True)
    return (first_own, second_own)


def solution(mesh):
    in_specs = (P("rows", None, None), P("rows", None), P("rows"), P("rows", None))
    out_specs = (P("rows", None), P("rows", None))
    return jax.shard_map(body, mesh=mesh, in_specs=in_specs, out_specs=out_specs, check_vma=False)
```

```python
import math

import jax
import jax.numpy as jnp
from jax import lax
from jax.experimental import pallas as pl
from jax.experimental.pallas import tpu as pltpu
from jax.sharding import PartitionSpec as P

score_gain = 0.4
norm_eps = 1e-06
HIGH = lax.Precision.HIGHEST


def line_table(lines):
    angle = 2.0 * math.pi * jnp.arange(lines).astype(jnp.float32) / lines
    return jnp.stack([jnp.cos(angle), jnp.sin(angle), jnp.cos(2.0 * angle)], axis=1)


def tile_kernel(a_ref, b_ref, w_ref, o_ref, s_ref):
    n = a_ref.shape[0]
    lines = w_ref.shape[1]
    width = a_ref.shape[1]
    groups = width // 128
    strips = lines // 8

    def per_image(a, carry):
        s_ref[...] = (
            lax.dot_general(
                b_ref[...], a_ref[a], (((1,), (1,)), ((), ())), preferred_element_type=jnp.float32
            )
            * score_gain
        )

        def per_partner(b, carry2):
            base = b * lines

            def col_max(r, m):
                start = pl.multiple_of(base + r * 8, 8)
                return jnp.maximum(m, s_ref[pl.ds(start, 8), :])

            m8 = lax.fori_loop(0, strips, col_max, jnp.full((8, width), -jnp.inf, jnp.float32))
            top = jnp.max(m8, axis=0, keepdims=True)
            top8 = jnp.broadcast_to(top, (8, width))

            def accumulate(r, acc):
                start = pl.multiple_of(base + r * 8, 8)
                e = jnp.exp(s_ref[pl.ds(start, 8), :] - top8)
                row = pl.multiple_of(r * 8, 8)
                out = [acc[0] + e]
                for q in range(3):
                    wq = w_ref[q, pl.ds(row, 8), :]
                    wide = jnp.concatenate([wq] * groups, axis=1)
                    out.append(acc[q + 1] + e * wide)
                return tuple(out)

            zero = jnp.zeros((8, width), jnp.float32)
            acc = lax.fori_loop(0, strips, accumulate, (zero, zero, zero, zero))
            o_ref[a, b, 0:1, :] = top
            for j in range(4):
                o_ref[a, b, j + 1 : j + 2, :] = jnp.sum(acc[j], axis=0, keepdims=True)
            return carry2

        lax.fori_loop(0, n, per_partner, 0)
        return carry

    lax.fori_loop(0, n, per_image, 0)


def pair_tile(own, other, table):
    count, lines, radii = own.shape
    padded = ((lines + 127) // 128) * 128
    own_p = jnp.pad(own, ((0, 0), (0, padded - lines), (0, 0)))
    wide = jnp.broadcast_to(jnp.transpose(table)[:, :, None], (3, lines, 128))
    stats = pl.pallas_call(
        tile_kernel,
        out_shape=jax.ShapeDtypeStruct((count, count, 8, padded), jnp.float32),
        in_specs=[pl.BlockSpec(memory_space=pltpu.VMEM)] * 3,
        out_specs=pl.BlockSpec(memory_space=pltpu.VMEM),
        scratch_shapes=[pltpu.VMEM((count * lines, padded), jnp.float32)],
        compiler_params=pltpu.CompilerParams(vmem_limit_bytes=48 * 1024 * 1024),
    )(own_p, other.reshape(count * lines, radii), wide)
    stats = stats[:, :, :, :lines]
    top = stats[:, :, 0, :]
    peak = jnp.max(top, axis=2, keepdims=True)
    scale = jnp.exp(top - peak)
    total = jnp.sum(scale * stats[:, :, 1, :], axis=2)
    sums = stats[:, :, 2:5, :] * scale[:, :, None, :]
    rel = jnp.einsum("lp,abql->abpq", table, sums, precision=HIGH)
    rel = rel / total[:, :, None, None]
    return jnp.transpose(rel, (2, 0, 3, 1)).reshape(3 * count, 3 * count)


def butterfly_sum(value, axes, size):
    bit = 1
    while bit < size:
        route = [(i, i ^ bit) for i in range(size)]
        value = value + lax.ppermute(value, axes, route)
        bit *= 2
    return value


def body(images, partners, counts, start):
    count, lines, radii = images.shape
    width = 3 * count
    slots = partners.shape[1]
    halo = slots // 2
    ncols = lax.axis_size("cols")
    nblk = lax.axis_size("rows")
    row = lax.axis_index("rows")
    column = lax.axis_index("cols")
    step = column + 1
    table = line_table(lines)

    axes = ("rows", "cols")
    route = []
    for i in range(nblk):
        for c in range(ncols):
            route.append((((i + c + 1) % nblk) * ncols + c, i * ncols + c))
    fetch = lambda v: lax.ppermute(v, axes, route)
    other = fetch(images)
    other_partners = fetch(partners)
    other_counts = fetch(counts)
    other_start = fetch(start)

    tile = pair_tile(images, other, table)

    slot_ids = jnp.arange(slots)
    plus = jnp.any((partners[0] == step + halo - 1) & (slot_ids < counts[0]))
    minus = jnp.any((other_partners[0] == halo - step) & (slot_ids < other_counts[0]))
    partner_row = (row + step) % nblk
    rows_ids = jnp.arange(nblk)
    at_own = (rows_ids == row)[:, None]
    at_other = (rows_ids == partner_row)[:, None]

    def spread(x_own, x_other):
        forward = jnp.where(plus, jnp.dot(tile, x_other, precision=HIGH), 0.0)
        backward = jnp.where(minus, jnp.dot(tile.T, x_own, precision=HIGH), 0.0)
        part = jnp.where(at_own, forward[None, :], 0.0) + jnp.where(at_other, backward[None, :], 0.0)
        return butterfly_sum(part, axes, nblk * ncols)

    entries = float(width * nblk)

    def normalize(raw):
        return raw / jnp.sqrt(jnp.sum(raw * raw) / entries + norm_eps)

    first_all = normalize(spread(start[0], other_start[0]))
    first_own = lax.dynamic_index_in_dim(first_all, row, 0, keepdims=True)
    first_other = lax.dynamic_index_in_dim(first_all, partner_row, 0, keepdims=False)
    second_all = normalize(spread(first_own[0], first_other))
    second_own = lax.dynamic_index_in_dim(second_all, row, 0, keepdims=True)
    return (first_own, second_own)


def solution(mesh):
    in_specs = (P("rows", None, None), P("rows", None), P("rows"), P("rows", None))
    out_specs = (P("rows", None), P("rows", None))
    return jax.shard_map(body, mesh=mesh, in_specs=in_specs, out_specs=out_specs, check_vma=False)
```

```python
import math

import jax
import jax.numpy as jnp
from jax import lax
from jax.experimental import pallas as pl
from jax.experimental.pallas import tpu as pltpu
from jax.sharding import PartitionSpec as P

score_gain = 0.4
norm_eps = 1e-06
HIGH = lax.Precision.HIGHEST


def line_table(lines):
    angle = 2.0 * math.pi * jnp.arange(lines).astype(jnp.float32) / lines
    return jnp.stack([jnp.cos(angle), jnp.sin(angle), jnp.cos(2.0 * angle)], axis=1)


def tile_kernel(a_ref, b_ref, w_ref, o_ref, s_ref):
    n = a_ref.shape[0]
    lines = w_ref.shape[1]
    width = a_ref.shape[1]
    groups = width // 128
    strips = lines // 8

    def per_image(a, carry):
        s_ref[...] = (
            lax.dot_general(
                b_ref[...], a_ref[a], (((1,), (1,)), ((), ())), preferred_element_type=jnp.float32
            )
            * score_gain
        )

        def per_partner(b, carry2):
            base = b * lines

            def col_max(r, m):
                start = pl.multiple_of(base + r * 8, 8)
                return jnp.maximum(m, s_ref[pl.ds(start, 8), :])

            m8 = lax.fori_loop(0, strips, col_max, jnp.full((8, width), -jnp.inf, jnp.float32), unroll=True)
            top = jnp.max(m8, axis=0, keepdims=True)
            top8 = jnp.broadcast_to(top, (8, width))

            def accumulate(r, acc):
                start = pl.multiple_of(base + r * 8, 8)
                e = jnp.exp(s_ref[pl.ds(start, 8), :] - top8)
                row = pl.multiple_of(r * 8, 8)
                out = [acc[0] + e]
                for q in range(3):
                    wq = w_ref[q, pl.ds(row, 8), :]
                    wide = jnp.concatenate([wq] * groups, axis=1)
                    out.append(acc[q + 1] + e * wide)
                return tuple(out)

            zero = jnp.zeros((8, width), jnp.float32)
            acc = lax.fori_loop(0, strips, accumulate, (zero, zero, zero, zero), unroll=True)
            o_ref[a, b, 0:1, :] = top
            for j in range(4):
                o_ref[a, b, j + 1 : j + 2, :] = jnp.sum(acc[j], axis=0, keepdims=True)
            return carry2

        lax.fori_loop(0, n, per_partner, 0)
        return carry

    lax.fori_loop(0, n, per_image, 0)


def pair_tile(own, other, table):
    count, lines, radii = own.shape
    padded = ((lines + 127) // 128) * 128
    own_p = jnp.pad(own, ((0, 0), (0, padded - lines), (0, 0)))
    wide = jnp.broadcast_to(jnp.transpose(table)[:, :, None], (3, lines, 128))
    stats = pl.pallas_call(
        tile_kernel,
        out_shape=jax.ShapeDtypeStruct((count, count, 8, padded), jnp.float32),
        in_specs=[pl.BlockSpec(memory_space=pltpu.VMEM)] * 3,
        out_specs=pl.BlockSpec(memory_space=pltpu.VMEM),
        scratch_shapes=[pltpu.VMEM((count * lines, padded), jnp.float32)],
        compiler_params=pltpu.CompilerParams(vmem_limit_bytes=48 * 1024 * 1024),
    )(own_p, other.reshape(count * lines, radii), wide)
    stats = stats[:, :, :, :lines]
    top = stats[:, :, 0, :]
    peak = jnp.max(top, axis=2, keepdims=True)
    scale = jnp.exp(top - peak)
    total = jnp.sum(scale * stats[:, :, 1, :], axis=2)
    sums = stats[:, :, 2:5, :] * scale[:, :, None, :]
    rel = jnp.einsum("lp,abql->abpq", table, sums, precision=HIGH)
    rel = rel / total[:, :, None, None]
    return jnp.transpose(rel, (2, 0, 3, 1)).reshape(3 * count, 3 * count)


def butterfly_sum(value, axes, size, bits):
    for bit in bits:
        route = [(i, i ^ bit) for i in range(size)]
        value = value + lax.ppermute(value, axes, route)
    return value


def body(images, partners, counts, start):
    count, lines, radii = images.shape
    width = 3 * count
    slots = partners.shape[1]
    halo = slots // 2
    ncols = lax.axis_size("cols")
    nblk = lax.axis_size("rows")
    size = nblk * ncols
    step = lax.axis_index("cols") + 1
    table = line_table(lines)

    axes = ("rows", "cols")
    route = []
    for i in range(nblk):
        for c in range(ncols):
            route.append((((i + c + 1) % nblk) * ncols + c, i * ncols + c))
    back = [(dst, src) for src, dst in route]
    fetch = lambda v: lax.ppermute(v, axes, route)
    other = fetch(images)
    other_partners = fetch(partners)
    other_counts = fetch(counts)
    other_start = fetch(start)

    tile = pair_tile(images, other, table)

    slot_ids = jnp.arange(slots)
    plus = jnp.any((partners[0] == step + halo - 1) & (slot_ids < counts[0]))
    minus = jnp.any((other_partners[0] == halo - step) & (slot_ids < other_counts[0]))
    col_bits = [1 << b for b in range(ncols.bit_length() - 1)]
    row_bits = [ncols << b for b in range(nblk.bit_length() - 1)]

    def apply(x_own, x_other):
        forward = jnp.where(plus, jnp.dot(tile, x_other, precision=HIGH), 0.0)
        backward = jnp.where(minus, jnp.dot(tile.T, x_own, precision=HIGH), 0.0)
        part = forward + lax.ppermute(backward, axes, back)
        return butterfly_sum(part, axes, size, col_bits)

    y1 = apply(start[0], other_start[0])
    z = apply(y1, fetch(y1))
    squares = jnp.stack([jnp.sum(y1 * y1), jnp.sum(z * z)])
    squares = butterfly_sum(squares, axes, size, row_bits)
    entries = float(width * nblk)
    s1 = jnp.sqrt(squares[0] / entries + norm_eps)
    first_vec = y1 / s1
    second_raw = z / s1
    s2 = jnp.sqrt(squares[1] / (s1 * s1) / entries + norm_eps)
    return (first_vec[None, :], (second_raw / s2)[None, :])


def solution(mesh):
    in_specs = (P("rows", None, None), P("rows", None), P("rows"), P("rows", None))
    out_specs = (P("rows", None), P("rows", None))
    return jax.shard_map(body, mesh=mesh, in_specs=in_specs, out_specs=out_specs, check_vma=False)
```

```python
import math

import jax
import jax.numpy as jnp
from jax import lax
from jax.experimental import pallas as pl
from jax.experimental.pallas import tpu as pltpu
from jax.sharding import PartitionSpec as P

score_gain = 0.4
norm_eps = 1e-06
HIGH = lax.Precision.HIGHEST


def line_table(lines):
    angle = 2.0 * math.pi * jnp.arange(lines).astype(jnp.float32) / lines
    return jnp.stack([jnp.cos(angle), jnp.sin(angle), jnp.cos(2.0 * angle)], axis=1)


def tile_kernel(a_ref, b_ref, w_ref, o_ref, s_ref):
    n = a_ref.shape[0]
    lines = w_ref.shape[1]
    nb = b_ref.shape[0] // lines
    width = a_ref.shape[1]
    groups = width // 128
    strips = lines // 8

    def per_image(a, carry):
        s_ref[...] = (
            lax.dot_general(
                b_ref[...], a_ref[a], (((1,), (1,)), ((), ())), preferred_element_type=jnp.float32
            )
            * score_gain
        )

        def per_partner(b, carry2):
            base = b * lines

            def col_max(r, m):
                start = pl.multiple_of(base + r * 8, 8)
                return jnp.maximum(m, s_ref[pl.ds(start, 8), :])

            m8 = lax.fori_loop(0, strips, col_max, jnp.full((8, width), -jnp.inf, jnp.float32), unroll=True)
            top = jnp.max(m8, axis=0, keepdims=True)
            top8 = jnp.broadcast_to(top, (8, width))

            def accumulate(r, acc):
                start = pl.multiple_of(base + r * 8, 8)
                e = jnp.exp(s_ref[pl.ds(start, 8), :] - top8)
                row = pl.multiple_of(r * 8, 8)
                out = [acc[0] + e]
                for q in range(3):
                    wq = w_ref[q, pl.ds(row, 8), :]
                    wide = jnp.concatenate([wq] * groups, axis=1)
                    out.append(acc[q + 1] + e * wide)
                return tuple(out)

            zero = jnp.zeros((8, width), jnp.float32)
            acc = lax.fori_loop(0, strips, accumulate, (zero, zero, zero, zero), unroll=True)
            o_ref[a, b, 0:1, :] = top
            for j in range(4):
                o_ref[a, b, j + 1 : j + 2, :] = jnp.sum(acc[j], axis=0, keepdims=True)
            return carry2

        lax.fori_loop(0, nb, per_partner, 0)
        return carry

    lax.fori_loop(0, n, per_image, 0)


def pair_stats(own_p, other, wide):
    count, padded, radii = own_p.shape
    part, lines, _ = other.shape
    flops = 2 * count * part * lines * padded * radii + 12 * count * part * lines * padded
    return pl.pallas_call(
        tile_kernel,
        out_shape=jax.ShapeDtypeStruct((count, part, 8, padded), jnp.float32),
        in_specs=[pl.BlockSpec(memory_space=pltpu.VMEM)] * 3,
        out_specs=pl.BlockSpec(memory_space=pltpu.VMEM),
        scratch_shapes=[pltpu.VMEM((part * lines, padded), jnp.float32)],
        compiler_params=pltpu.CompilerParams(vmem_limit_bytes=48 * 1024 * 1024),
        cost_estimate=pl.CostEstimate(
            flops=flops, transcendentals=count * part * lines * padded, bytes_accessed=2 * 1024 * 1024
        ),
    )(own_p, other.reshape(part * lines, radii), wide)


def pair_tile(own, others, table):
    count, lines, radii = own.shape
    padded = ((lines + 127) // 128) * 128
    own_p = jnp.pad(own, ((0, 0), (0, padded - lines), (0, 0)))
    wide = jnp.broadcast_to(jnp.transpose(table)[:, :, None], (3, lines, 128))
    stats = jnp.concatenate([pair_stats(own_p, other, wide) for other in others], axis=1)
    stats = stats[:, :, :, :lines]
    top = stats[:, :, 0, :]
    peak = jnp.max(top, axis=2, keepdims=True)
    scale = jnp.exp(top - peak)
    total = jnp.sum(scale * stats[:, :, 1, :], axis=2)
    sums = stats[:, :, 2:5, :] * scale[:, :, None, :]
    rel = jnp.einsum("lp,abql->abpq", table, sums, precision=HIGH)
    rel = rel / total[:, :, None, None]
    return jnp.transpose(rel, (2, 0, 3, 1)).reshape(3 * count, 3 * count)


def butterfly_sum(value, axes, size, bits):
    for bit in bits:
        route = [(i, i ^ bit) for i in range(size)]
        value = value + lax.ppermute(value, axes, route)
    return value


def body(images, partners, counts, start):
    count, lines, radii = images.shape
    width = 3 * count
    slots = partners.shape[1]
    halo = slots // 2
    ncols = lax.axis_size("cols")
    nblk = lax.axis_size("rows")
    size = nblk * ncols
    step = lax.axis_index("cols") + 1
    table = line_table(lines)

    axes = ("rows", "cols")
    route = []
    for i in range(nblk):
        for c in range(ncols):
            route.append((((i + c + 1) % nblk) * ncols + c, i * ncols + c))
    back = [(dst, src) for src, dst in route]
    fetch = lambda v: lax.ppermute(v, axes, route)
    half = count // 2
    others = [fetch(images[:half]), fetch(images[half:])]
    other_partners = fetch(partners)
    other_counts = fetch(counts)
    other_start = fetch(start)

    tile = pair_tile(images, others, table)

    slot_ids = jnp.arange(slots)
    plus = jnp.any((partners[0] == step + halo - 1) & (slot_ids < counts[0]))
    minus = jnp.any((other_partners[0] == halo - step) & (slot_ids < other_counts[0]))
    col_bits = [1 << b for b in range(ncols.bit_length() - 1)]
    row_bits = [ncols << b for b in range(nblk.bit_length() - 1)]

    def apply(x_own, x_other):
        forward = jnp.where(plus, jnp.dot(tile, x_other, precision=HIGH), 0.0)
        backward = jnp.where(minus, jnp.dot(tile.T, x_own, precision=HIGH), 0.0)
        part = forward + lax.ppermute(backward, axes, back)
        return butterfly_sum(part, axes, size, col_bits)

    y1 = apply(start[0], other_start[0])
    z = apply(y1, fetch(y1))
    squares = jnp.stack([jnp.sum(y1 * y1), jnp.sum(z * z)])
    squares = butterfly_sum(squares, axes, size, row_bits)
    entries = float(width * nblk)
    s1 = jnp.sqrt(squares[0] / entries + norm_eps)
    first_vec = y1 / s1
    second_raw = z / s1
    s2 = jnp.sqrt(squares[1] / (s1 * s1) / entries + norm_eps)
    return (first_vec[None, :], (second_raw / s2)[None, :])


def solution(mesh):
    in_specs = (P("rows", None, None), P("rows", None), P("rows"), P("rows", None))
    out_specs = (P("rows", None), P("rows", None))
    return jax.shard_map(body, mesh=mesh, in_specs=in_specs, out_specs=out_specs, check_vma=False)
```

```python
import math

import jax
import jax.numpy as jnp
from jax import lax
from jax.experimental import pallas as pl
from jax.experimental.pallas import tpu as pltpu
from jax.sharding import PartitionSpec as P

score_gain = 0.4
norm_eps = 1e-06
HIGH = lax.Precision.HIGHEST


def line_table(lines):
    angle = 2.0 * math.pi * jnp.arange(lines).astype(jnp.float32) / lines
    return jnp.stack([jnp.cos(angle), jnp.sin(angle), jnp.cos(2.0 * angle)], axis=1)


def tile_kernel(a_ref, b_ref, w_ref, o_ref, s_ref):
    n = a_ref.shape[0]
    lines = w_ref.shape[1]
    nb = b_ref.shape[0] // lines
    width = a_ref.shape[1]
    groups = width // 128
    strips = lines // 8

    def per_image(a, carry):
        s_ref[...] = (
            lax.dot_general(
                b_ref[...], a_ref[a], (((1,), (1,)), ((), ())), preferred_element_type=jnp.float32
            )
            * score_gain
        )

        def per_partner(b, carry2):
            base = b * lines

            def col_max(r, m):
                start = pl.multiple_of(base + r * 8, 8)
                return jnp.maximum(m, s_ref[pl.ds(start, 8), :])

            m8 = lax.fori_loop(0, strips, col_max, jnp.full((8, width), -jnp.inf, jnp.float32), unroll=True)
            top = jnp.max(m8, axis=0, keepdims=True)
            top8 = jnp.broadcast_to(top, (8, width))

            def accumulate(r, acc):
                start = pl.multiple_of(base + r * 8, 8)
                e = jnp.exp(s_ref[pl.ds(start, 8), :] - top8)
                row = pl.multiple_of(r * 8, 8)
                out = [acc[0] + e]
                for q in range(3):
                    wq = w_ref[q, pl.ds(row, 8), :]
                    wide = jnp.concatenate([wq] * groups, axis=1)
                    out.append(acc[q + 1] + e * wide)
                return tuple(out)

            zero = jnp.zeros((8, width), jnp.float32)
            acc = lax.fori_loop(0, strips, accumulate, (zero, zero, zero, zero), unroll=True)
            o_ref[a, b, 0:1, :] = top
            for j in range(4):
                o_ref[a, b, j + 1 : j + 2, :] = jnp.sum(acc[j], axis=0, keepdims=True)
            return carry2

        lax.fori_loop(0, nb, per_partner, 0)
        return carry

    lax.fori_loop(0, n, per_image, 0)


def pair_stats(own_p, other, wide):
    count, padded, radii = own_p.shape
    part, lines, _ = other.shape
    flops = 2 * count * part * lines * padded * radii + 12 * count * part * lines * padded
    return pl.pallas_call(
        tile_kernel,
        out_shape=jax.ShapeDtypeStruct((count, part, 8, padded), jnp.float32),
        in_specs=[pl.BlockSpec(memory_space=pltpu.VMEM)] * 3,
        out_specs=pl.BlockSpec(memory_space=pltpu.VMEM),
        scratch_shapes=[pltpu.VMEM((part * lines, padded), jnp.float32)],
        compiler_params=pltpu.CompilerParams(vmem_limit_bytes=48 * 1024 * 1024),
        cost_estimate=pl.CostEstimate(
            flops=flops, transcendentals=count * part * lines * padded, bytes_accessed=2 * 1024 * 1024
        ),
    )(own_p, other.reshape(part * lines, radii), wide)


def pair_tile(own, others, table):
    count, lines, radii = own.shape
    padded = ((lines + 127) // 128) * 128
    own_p = jnp.pad(own, ((0, 0), (0, padded - lines), (0, 0)))
    wide = jnp.broadcast_to(jnp.transpose(table)[:, :, None], (3, lines, 128))
    stats = jnp.concatenate([pair_stats(own_p, other, wide) for other in others], axis=1)
    stats = stats[:, :, :, :lines]
    top = stats[:, :, 0, :]
    peak = jnp.max(top, axis=2, keepdims=True)
    scale = jnp.exp(top - peak)
    total = jnp.sum(scale * stats[:, :, 1, :], axis=2)
    sums = stats[:, :, 2:5, :] * scale[:, :, None, :]
    rel = jnp.einsum("lp,abql->abpq", table, sums, precision=HIGH)
    rel = rel / total[:, :, None, None]
    return jnp.transpose(rel, (2, 0, 3, 1)).reshape(3 * count, 3 * count)


def butterfly_sum(value, axes, size, bits):
    for bit in bits:
        route = [(i, i ^ bit) for i in range(size)]
        value = value + lax.ppermute(value, axes, route)
    return value


def body(images, partners, counts, start):
    count, lines, radii = images.shape
    width = 3 * count
    slots = partners.shape[1]
    halo = slots // 2
    ncols = lax.axis_size("cols")
    nblk = lax.axis_size("rows")
    size = nblk * ncols
    step = lax.axis_index("cols") + 1
    table = line_table(lines)

    axes = ("rows", "cols")
    route = []
    for i in range(nblk):
        for c in range(ncols):
            route.append((((i + c + 1) % nblk) * ncols + c, i * ncols + c))
    back = [(dst, src) for src, dst in route]
    fetch = lambda v: lax.ppermute(v, axes, route)
    half = count // 2
    first_half = fetch(images[:half])
    second_src, first_half = lax.optimization_barrier((images[half:], first_half))
    others = [first_half, fetch(second_src)]
    other_partners = fetch(partners)
    other_counts = fetch(counts)
    other_start = fetch(start)

    tile = pair_tile(images, others, table)

    slot_ids = jnp.arange(slots)
    plus = jnp.any((partners[0] == step + halo - 1) & (slot_ids < counts[0]))
    minus = jnp.any((other_partners[0] == halo - step) & (slot_ids < other_counts[0]))
    col_bits = [1 << b for b in range(ncols.bit_length() - 1)]
    row_bits = [ncols << b for b in range(nblk.bit_length() - 1)]

    def apply(x_own, x_other):
        forward = jnp.where(plus, jnp.dot(tile, x_other, precision=HIGH), 0.0)
        backward = jnp.where(minus, jnp.dot(tile.T, x_own, precision=HIGH), 0.0)
        part = forward + lax.ppermute(backward, axes, back)
        return butterfly_sum(part, axes, size, col_bits)

    y1 = apply(start[0], other_start[0])
    z = apply(y1, fetch(y1))
    squares = jnp.stack([jnp.sum(y1 * y1), jnp.sum(z * z)])
    squares = butterfly_sum(squares, axes, size, row_bits)
    entries = float(width * nblk)
    s1 = jnp.sqrt(squares[0] / entries + norm_eps)
    first_vec = y1 / s1
    second_raw = z / s1
    s2 = jnp.sqrt(squares[1] / (s1 * s1) / entries + norm_eps)
    return (first_vec[None, :], (second_raw / s2)[None, :])


def solution(mesh):
    in_specs = (P("rows", None, None), P("rows", None), P("rows"), P("rows", None))
    out_specs = (P("rows", None), P("rows", None))
    return jax.shard_map(body, mesh=mesh, in_specs=in_specs, out_specs=out_specs, check_vma=False)
```

```python
import math

import jax
import jax.numpy as jnp
from jax import lax
from jax.experimental import pallas as pl
from jax.experimental.pallas import tpu as pltpu
from jax.sharding import PartitionSpec as P

score_gain = 0.4
norm_eps = 1e-06
HIGH = lax.Precision.HIGHEST


def line_table(lines):
    angle = 2.0 * math.pi * jnp.arange(lines).astype(jnp.float32) / lines
    return jnp.stack([jnp.cos(angle), jnp.sin(angle), jnp.cos(2.0 * angle)], axis=1)


def tile_kernel(a_ref, b_ref, w_ref, o_ref, s_ref):
    n = a_ref.shape[0]
    lines = w_ref.shape[1]
    nb = b_ref.shape[0] // lines
    width = a_ref.shape[1]
    groups = width // 128
    strips = lines // 8

    def per_image(a, carry):
        s_ref[...] = (
            lax.dot_general(
                b_ref[...], a_ref[a], (((1,), (1,)), ((), ())), preferred_element_type=jnp.float32
            )
            * score_gain
        )

        def per_partner(b, carry2):
            base = b * lines

            def col_max(r, m):
                start = pl.multiple_of(base + r * 8, 8)
                return jnp.maximum(m, s_ref[pl.ds(start, 8), :])

            m8 = lax.fori_loop(0, strips, col_max, jnp.full((8, width), -jnp.inf, jnp.float32), unroll=True)
            top = jnp.max(m8, axis=0, keepdims=True)
            top8 = jnp.broadcast_to(top, (8, width))

            def accumulate(r, acc):
                start = pl.multiple_of(base + r * 8, 8)
                e = jnp.exp(s_ref[pl.ds(start, 8), :] - top8)
                row = pl.multiple_of(r * 8, 8)
                out = [acc[0] + e]
                for q in range(3):
                    wq = w_ref[q, pl.ds(row, 8), :]
                    wide = jnp.concatenate([wq] * groups, axis=1)
                    out.append(acc[q + 1] + e * wide)
                return tuple(out)

            zero = jnp.zeros((8, width), jnp.float32)
            acc = lax.fori_loop(0, strips, accumulate, (zero, zero, zero, zero), unroll=True)
            o_ref[a, b, 0:1, :] = top
            for j in range(4):
                o_ref[a, b, j + 1 : j + 2, :] = jnp.sum(acc[j], axis=0, keepdims=True)
            return carry2

        lax.fori_loop(0, nb, per_partner, 0)
        return carry

    lax.fori_loop(0, n, per_image, 0)


def pair_stats(own_p, other, wide):
    count, padded, radii = own_p.shape
    part, lines, _ = other.shape
    flops = 2 * count * part * lines * padded * radii + 12 * count * part * lines * padded
    return pl.pallas_call(
        tile_kernel,
        out_shape=jax.ShapeDtypeStruct((count, part, 8, padded), jnp.float32),
        in_specs=[pl.BlockSpec(memory_space=pltpu.VMEM)] * 3,
        out_specs=pl.BlockSpec(memory_space=pltpu.VMEM),
        scratch_shapes=[pltpu.VMEM((part * lines, padded), jnp.float32)],
        compiler_params=pltpu.CompilerParams(vmem_limit_bytes=48 * 1024 * 1024),
        cost_estimate=pl.CostEstimate(
            flops=flops, transcendentals=count * part * lines * padded, bytes_accessed=2 * 1024 * 1024
        ),
    )(own_p, other.reshape(part * lines, radii), wide)


def pair_tile(own, others, table):
    count, lines, radii = own.shape
    padded = ((lines + 127) // 128) * 128
    own_p = jnp.pad(own, ((0, 0), (0, padded - lines), (0, 0)))
    wide = jnp.broadcast_to(jnp.transpose(table)[:, :, None], (3, lines, 128))
    stats = jnp.concatenate([pair_stats(own_p, other, wide) for other in others], axis=1)
    stats = stats[:, :, :, :lines]
    top = stats[:, :, 0, :]
    peak = jnp.max(top, axis=2, keepdims=True)
    scale = jnp.exp(top - peak)
    total = jnp.sum(scale * stats[:, :, 1, :], axis=2)
    sums = stats[:, :, 2:5, :] * scale[:, :, None, :]
    rel = jnp.einsum("lp,abql->abpq", table, sums, precision=HIGH)
    rel = rel / total[:, :, None, None]
    return jnp.transpose(rel, (2, 0, 3, 1)).reshape(3 * count, 3 * count)


def butterfly_sum(value, axes, size, bits):
    for bit in bits:
        route = [(i, i ^ bit) for i in range(size)]
        value = value + lax.ppermute(value, axes, route)
    return value


def body(images, partners, counts, start):
    count, lines, radii = images.shape
    width = 3 * count
    slots = partners.shape[1]
    halo = slots // 2
    ncols = lax.axis_size("cols")
    nblk = lax.axis_size("rows")
    size = nblk * ncols
    step = lax.axis_index("cols") + 1
    table = line_table(lines)

    axes = ("rows", "cols")
    route = []
    for i in range(nblk):
        for c in range(ncols):
            route.append((((i + c + 1) % nblk) * ncols + c, i * ncols + c))
    back = [(dst, src) for src, dst in route]
    fetch = lambda v: lax.ppermute(v, axes, route)
    half = count // 2
    first_half = fetch(images[:half])
    second_src, first_half = lax.optimization_barrier((images[half:], first_half))
    others = [first_half, fetch(second_src)]
    packed = jnp.concatenate(
        [partners[0].astype(jnp.float32), counts.astype(jnp.float32), start[0]]
    )
    other_packed = fetch(packed)
    other_partners = other_packed[:slots]
    other_counts = other_packed[slots]
    other_start = other_packed[slots + 1 :]

    tile = pair_tile(images, others, table)

    slot_ids = jnp.arange(slots)
    plus = jnp.any((partners[0] == step + halo - 1) & (slot_ids < counts[0]))
    minus = jnp.any((other_partners == (halo - step).astype(jnp.float32)) & (slot_ids < other_counts))
    col_bits = [1 << b for b in range(ncols.bit_length() - 1)]

    def apply(x_own, x_other):
        forward = jnp.where(plus, jnp.dot(tile, x_other, precision=HIGH), 0.0)
        backward = jnp.where(minus, jnp.dot(tile.T, x_own, precision=HIGH), 0.0)
        part = forward + lax.ppermute(backward, axes, back)
        return butterfly_sum(part, axes, size, col_bits)

    y1 = apply(start[0], other_start)
    z = apply(y1, fetch(y1))
    squares = jnp.stack([jnp.sum(y1 * y1), jnp.sum(z * z)])
    squares = jnp.sum(lax.all_to_all(jnp.broadcast_to(squares, (nblk, 2)), "rows", 0, 0, tiled=True), axis=0)
    entries = float(width * nblk)
    s1 = jnp.sqrt(squares[0] / entries + norm_eps)
    first_vec = y1 / s1
    second_raw = z / s1
    s2 = jnp.sqrt(squares[1] / (s1 * s1) / entries + norm_eps)
    return (first_vec[None, :], (second_raw / s2)[None, :])


def solution(mesh):
    in_specs = (P("rows", None, None), P("rows", None), P("rows"), P("rows", None))
    out_specs = (P("rows", None), P("rows", None))
    return jax.shard_map(body, mesh=mesh, in_specs=in_specs, out_specs=out_specs, check_vma=False)
```

```python
import math

import jax
import jax.numpy as jnp
from jax import lax
from jax.experimental import pallas as pl
from jax.experimental.pallas import tpu as pltpu
from jax.sharding import PartitionSpec as P

score_gain = 0.4
norm_eps = 1e-06
HIGH = lax.Precision.HIGHEST


def line_table(lines):
    angle = 2.0 * math.pi * jnp.arange(lines).astype(jnp.float32) / lines
    return jnp.stack([jnp.cos(angle), jnp.sin(angle), jnp.cos(2.0 * angle)], axis=1)


def tile_kernel(a_ref, b_ref, w_ref, o_ref, s_ref):
    n = a_ref.shape[0]
    lines = w_ref.shape[1]
    nb = b_ref.shape[0] // lines
    width = a_ref.shape[1]
    groups = width // 128
    strips = lines // 8

    def per_image(a, carry):
        s_ref[...] = (
            lax.dot_general(
                b_ref[...], a_ref[a], (((1,), (1,)), ((), ())), preferred_element_type=jnp.float32
            )
            * score_gain
        )

        def per_partner(b, carry2):
            base = b * lines

            def col_max(r, m):
                start = pl.multiple_of(base + r * 8, 8)
                return jnp.maximum(m, s_ref[pl.ds(start, 8), :])

            m8 = lax.fori_loop(0, strips, col_max, jnp.full((8, width), -jnp.inf, jnp.float32), unroll=True)
            top = jnp.max(m8, axis=0, keepdims=True)
            top8 = jnp.broadcast_to(top, (8, width))

            def accumulate(r, acc):
                start = pl.multiple_of(base + r * 8, 8)
                e = jnp.exp(s_ref[pl.ds(start, 8), :] - top8)
                row = pl.multiple_of(r * 8, 8)
                out = [acc[0] + e]
                for q in range(3):
                    wq = w_ref[q, pl.ds(row, 8), :]
                    wide = jnp.concatenate([wq] * groups, axis=1)
                    out.append(acc[q + 1] + e * wide)
                return tuple(out)

            zero = jnp.zeros((8, width), jnp.float32)
            acc = lax.fori_loop(0, strips, accumulate, (zero, zero, zero, zero), unroll=True)
            o_ref[a, b, 0:1, :] = top
            for j in range(4):
                o_ref[a, b, j + 1 : j + 2, :] = jnp.sum(acc[j], axis=0, keepdims=True)
            return carry2

        lax.fori_loop(0, nb, per_partner, 0)
        return carry

    lax.fori_loop(0, n, per_image, 0)


def pair_stats(own_p, other, wide):
    count, padded, radii = own_p.shape
    part, lines, _ = other.shape
    flops = 2 * count * part * lines * padded * radii + 12 * count * part * lines * padded
    return pl.pallas_call(
        tile_kernel,
        out_shape=jax.ShapeDtypeStruct((count, part, 8, padded), jnp.float32),
        in_specs=[pl.BlockSpec(memory_space=pltpu.VMEM)] * 3,
        out_specs=pl.BlockSpec(memory_space=pltpu.VMEM),
        scratch_shapes=[pltpu.VMEM((part * lines, padded), jnp.float32)],
        compiler_params=pltpu.CompilerParams(vmem_limit_bytes=48 * 1024 * 1024),
        cost_estimate=pl.CostEstimate(
            flops=flops, transcendentals=count * part * lines * padded, bytes_accessed=2 * 1024 * 1024
        ),
    )(own_p, other.reshape(part * lines, radii), wide)


def pair_tile(own, others, table):
    count, lines, radii = own.shape
    padded = ((lines + 127) // 128) * 128
    own_p = jnp.pad(own, ((0, 0), (0, padded - lines), (0, 0)))
    wide = jnp.broadcast_to(jnp.transpose(table)[:, :, None], (3, lines, 128))
    stats = jnp.concatenate([pair_stats(own_p, other, wide) for other in others], axis=1)
    stats = stats[:, :, :, :lines]
    top = stats[:, :, 0, :]
    peak = jnp.max(top, axis=2, keepdims=True)
    scale = jnp.exp(top - peak)
    total = jnp.sum(scale * stats[:, :, 1, :], axis=2)
    sums = stats[:, :, 2:5, :] * scale[:, :, None, :]
    rel = jnp.einsum("lp,abql->abpq", table, sums, precision=HIGH)
    rel = rel / total[:, :, None, None]
    return jnp.transpose(rel, (2, 0, 3, 1)).reshape(3 * count, 3 * count)


def butterfly_sum(value, axes, size, bits):
    for bit in bits:
        route = [(i, i ^ bit) for i in range(size)]
        value = value + lax.ppermute(value, axes, route)
    return value


def body(images, partners, counts, start):
    count, lines, radii = images.shape
    width = 3 * count
    slots = partners.shape[1]
    halo = slots // 2
    ncols = lax.axis_size("cols")
    nblk = lax.axis_size("rows")
    size = nblk * ncols
    step = lax.axis_index("cols") + 1
    table = line_table(lines)

    axes = ("rows", "cols")
    route = []
    for i in range(nblk):
        for c in range(ncols):
            route.append((((i + c + 1) % nblk) * ncols + c, i * ncols + c))
    back = [(dst, src) for src, dst in route]
    mirror = []
    for i in range(nblk):
        for c in range(ncols):
            mirror.append((((i + c + 1) % nblk) * ncols + (ncols - 1 - c), i * ncols + c))
    fetch = lambda v: lax.ppermute(v, axes, route)
    half = count // 2
    first_half = fetch(images[:half])
    second_src, first_half = lax.optimization_barrier((images[half:], first_half))
    others = [first_half, lax.ppermute(second_src, axes, mirror)]
    packed = jnp.concatenate(
        [partners[0].astype(jnp.float32), counts.astype(jnp.float32), start[0]]
    )
    other_packed = fetch(packed)
    other_partners = other_packed[:slots]
    other_counts = other_packed[slots]
    other_start = other_packed[slots + 1 :]

    tile = pair_tile(images, others, table)

    slot_ids = jnp.arange(slots)
    plus = jnp.any((partners[0] == step + halo - 1) & (slot_ids < counts[0]))
    minus = jnp.any((other_partners == (halo - step).astype(jnp.float32)) & (slot_ids < other_counts))
    col_bits = [1 << b for b in range(ncols.bit_length() - 1)]

    def apply(x_own, x_other):
        forward = jnp.where(plus, jnp.dot(tile, x_other, precision=HIGH), 0.0)
        backward = jnp.where(minus, jnp.dot(tile.T, x_own, precision=HIGH), 0.0)
        part = forward + lax.ppermute(backward, axes, back)
        return butterfly_sum(part, axes, size, col_bits)

    y1 = apply(start[0], other_start)
    z = apply(y1, fetch(y1))
    squares = jnp.stack([jnp.sum(y1 * y1), jnp.sum(z * z)])
    squares = jnp.sum(lax.all_to_all(jnp.broadcast_to(squares, (nblk, 2)), "rows", 0, 0, tiled=True), axis=0)
    entries = float(width * nblk)
    s1 = jnp.sqrt(squares[0] / entries + norm_eps)
    first_vec = y1 / s1
    second_raw = z / s1
    s2 = jnp.sqrt(squares[1] / (s1 * s1) / entries + norm_eps)
    return (first_vec[None, :], (second_raw / s2)[None, :])


def solution(mesh):
    in_specs = (P("rows", None, None), P("rows", None), P("rows"), P("rows", None))
    out_specs = (P("rows", None), P("rows", None))
    return jax.shard_map(body, mesh=mesh, in_specs=in_specs, out_specs=out_specs, check_vma=False)
```

```python
import math

import jax
import jax.numpy as jnp
from jax import lax
from jax.experimental import pallas as pl
from jax.experimental.pallas import tpu as pltpu
from jax.sharding import PartitionSpec as P

score_gain = 0.4
norm_eps = 1e-06
HIGH = lax.Precision.HIGHEST


def line_table(lines):
    angle = 2.0 * math.pi * jnp.arange(lines).astype(jnp.float32) / lines
    return jnp.stack([jnp.cos(angle), jnp.sin(angle), jnp.cos(2.0 * angle)], axis=1)


def tile_kernel(a_ref, b_ref, w_ref, o_ref, s_ref):
    n = a_ref.shape[0]
    lines = w_ref.shape[1]
    nb = b_ref.shape[0] // lines
    width = a_ref.shape[1]
    groups = width // 128
    strips = lines // 8

    def per_image(a, carry):
        s_ref[...] = (
            lax.dot_general(
                b_ref[...], a_ref[a], (((1,), (1,)), ((), ())), preferred_element_type=jnp.float32
            )
            * score_gain
        )

        def per_partner(b, carry2):
            base = b * lines

            def col_max(r, m):
                start = pl.multiple_of(base + r * 8, 8)
                return jnp.maximum(m, s_ref[pl.ds(start, 8), :])

            m8 = lax.fori_loop(0, strips, col_max, jnp.full((8, width), -jnp.inf, jnp.float32), unroll=True)
            top = jnp.max(m8, axis=0, keepdims=True)
            top8 = jnp.broadcast_to(top, (8, width))

            def accumulate(r, acc):
                start = pl.multiple_of(base + r * 8, 8)
                e = jnp.exp(s_ref[pl.ds(start, 8), :] - top8)
                row = pl.multiple_of(r * 8, 8)
                out = [acc[0] + e]
                for q in range(3):
                    wq = w_ref[q, pl.ds(row, 8), :]
                    wide = jnp.concatenate([wq] * groups, axis=1)
                    out.append(acc[q + 1] + e * wide)
                return tuple(out)

            zero = jnp.zeros((8, width), jnp.float32)
            acc = lax.fori_loop(0, strips, accumulate, (zero, zero, zero, zero), unroll=True)
            o_ref[a, b, 0:1, :] = top
            for j in range(4):
                o_ref[a, b, j + 1 : j + 2, :] = jnp.sum(acc[j], axis=0, keepdims=True)
            return carry2

        lax.fori_loop(0, nb, per_partner, 0)
        return carry

    lax.fori_loop(0, n, per_image, 0)


def pair_stats(own_p, other, wide):
    count, padded, radii = own_p.shape
    part, lines, _ = other.shape
    flops = 2 * count * part * lines * padded * radii + 12 * count * part * lines * padded
    return pl.pallas_call(
        tile_kernel,
        out_shape=jax.ShapeDtypeStruct((count, part, 8, padded), jnp.float32),
        in_specs=[pl.BlockSpec(memory_space=pltpu.VMEM)] * 3,
        out_specs=pl.BlockSpec(memory_space=pltpu.VMEM),
        scratch_shapes=[pltpu.VMEM((part * lines, padded), jnp.float32)],
        compiler_params=pltpu.CompilerParams(vmem_limit_bytes=48 * 1024 * 1024),
        cost_estimate=pl.CostEstimate(
            flops=flops, transcendentals=count * part * lines * padded, bytes_accessed=2 * 1024 * 1024
        ),
    )(own_p, other.reshape(part * lines, radii), wide)


def pair_tile(own, others, table):
    count, lines, radii = own.shape
    padded = ((lines + 127) // 128) * 128
    own_p = jnp.pad(own, ((0, 0), (0, padded - lines), (0, 0)))
    wide = jnp.broadcast_to(jnp.transpose(table)[:, :, None], (3, lines, 128))
    stats = jnp.concatenate([pair_stats(own_p, other, wide) for other in others], axis=1)
    stats = stats[:, :, :, :lines]
    top = stats[:, :, 0, :]
    peak = jnp.max(top, axis=2, keepdims=True)
    scale = jnp.exp(top - peak)
    total = jnp.sum(scale * stats[:, :, 1, :], axis=2)
    sums = stats[:, :, 2:5, :] * scale[:, :, None, :]
    rel = jnp.einsum("lp,abql->abpq", table, sums, precision=HIGH)
    rel = rel / total[:, :, None, None]
    return jnp.transpose(rel, (2, 0, 3, 1)).reshape(3 * count, 3 * count)


def butterfly_sum(value, axes, size, bits):
    for bit in bits:
        route = [(i, i ^ bit) for i in range(size)]
        value = value + lax.ppermute(value, axes, route)
    return value


def body(images, partners, counts, start):
    count, lines, radii = images.shape
    width = 3 * count
    slots = partners.shape[1]
    halo = slots // 2
    ncols = lax.axis_size("cols")
    nblk = lax.axis_size("rows")
    size = nblk * ncols
    step = lax.axis_index("cols") + 1
    table = line_table(lines)

    axes = ("rows", "cols")
    route = []
    for i in range(nblk):
        for c in range(ncols):
            route.append((((i + c + 1) % nblk) * ncols + c, i * ncols + c))
    back = [(dst, src) for src, dst in route]
    mirror = []
    for i in range(nblk):
        for c in range(ncols):
            mirror.append((((i + c + 1) % nblk) * ncols + (ncols - 1 - c), i * ncols + c))
    fetch = lambda v: lax.ppermute(v, axes, route)
    half = count // 2
    others = [fetch(images[:half]), lax.ppermute(images[half:], axes, mirror)]
    packed = jnp.concatenate(
        [partners[0].astype(jnp.float32), counts.astype(jnp.float32), start[0]]
    )
    other_packed = fetch(packed)
    other_partners = other_packed[:slots]
    other_counts = other_packed[slots]
    other_start = other_packed[slots + 1 :]

    tile = pair_tile(images, others, table)

    slot_ids = jnp.arange(slots)
    plus = jnp.any((partners[0] == step + halo - 1) & (slot_ids < counts[0]))
    minus = jnp.any((other_partners == (halo - step).astype(jnp.float32)) & (slot_ids < other_counts))
    col_bits = [1 << b for b in range(ncols.bit_length() - 1)]

    def apply(x_own, x_other):
        forward = jnp.where(plus, jnp.dot(tile, x_other, precision=HIGH), 0.0)
        backward = jnp.where(minus, jnp.dot(tile.T, x_own, precision=HIGH), 0.0)
        part = forward + lax.ppermute(backward, axes, back)
        return butterfly_sum(part, axes, size, col_bits)

    y1 = apply(start[0], other_start)
    z = apply(y1, fetch(y1))
    squares = jnp.stack([jnp.sum(y1 * y1), jnp.sum(z * z)])
    squares = jnp.sum(lax.all_to_all(jnp.broadcast_to(squares, (nblk, 2)), "rows", 0, 0, tiled=True), axis=0)
    entries = float(width * nblk)
    s1 = jnp.sqrt(squares[0] / entries + norm_eps)
    first_vec = y1 / s1
    second_raw = z / s1
    s2 = jnp.sqrt(squares[1] / (s1 * s1) / entries + norm_eps)
    return (first_vec[None, :], (second_raw / s2)[None, :])


def solution(mesh):
    in_specs = (P("rows", None, None), P("rows", None), P("rows"), P("rows", None))
    out_specs = (P("rows", None), P("rows", None))
    return jax.shard_map(body, mesh=mesh, in_specs=in_specs, out_specs=out_specs, check_vma=False)
```

```python
import math

import jax
import jax.numpy as jnp
from jax import lax
from jax.experimental import pallas as pl
from jax.experimental.pallas import tpu as pltpu
from jax.sharding import PartitionSpec as P

score_gain = 0.4
norm_eps = 1e-06
HIGH = lax.Precision.HIGHEST
LOG2E = 1.4426950408889634


def line_table(lines):
    angle = 2.0 * math.pi * jnp.arange(lines).astype(jnp.float32) / lines
    return jnp.stack([jnp.cos(angle), jnp.sin(angle), jnp.cos(2.0 * angle)], axis=1)


def tile_kernel(a_ref, b_ref, w_ref, o_ref, s_ref):
    n = a_ref.shape[0]
    lines = w_ref.shape[1]
    nb = b_ref.shape[0] // lines
    width = a_ref.shape[1]
    groups = width // 128
    strips = lines // 8

    def per_image(a, carry):
        s_ref[...] = (
            lax.dot_general(
                b_ref[...], a_ref[a], (((1,), (1,)), ((), ())), preferred_element_type=jnp.float32
            )
            * (score_gain * LOG2E)
        )

        def per_partner(b, carry2):
            base = b * lines

            def col_max(r, m):
                start = pl.multiple_of(base + r * 8, 8)
                return jnp.maximum(m, s_ref[pl.ds(start, 8), :])

            m8 = lax.fori_loop(0, strips, col_max, jnp.full((8, width), -jnp.inf, jnp.float32), unroll=True)
            top = jnp.max(m8, axis=0, keepdims=True)
            top8 = jnp.broadcast_to(top, (8, width))

            def accumulate(r, acc):
                start = pl.multiple_of(base + r * 8, 8)
                e = jnp.exp2(s_ref[pl.ds(start, 8), :] - top8)
                row = pl.multiple_of(r * 8, 8)
                out = [acc[0] + e]
                for q in range(3):
                    wq = w_ref[q, pl.ds(row, 8), :]
                    wide = jnp.concatenate([wq] * groups, axis=1)
                    out.append(acc[q + 1] + e * wide)
                return tuple(out)

            zero = jnp.zeros((8, width), jnp.float32)
            acc = lax.fori_loop(0, strips, accumulate, (zero, zero, zero, zero), unroll=True)
            o_ref[a, b, 0:1, :] = top
            for j in range(4):
                o_ref[a, b, j + 1 : j + 2, :] = jnp.sum(acc[j], axis=0, keepdims=True)
            return carry2

        lax.fori_loop(0, nb, per_partner, 0)
        return carry

    lax.fori_loop(0, n, per_image, 0)


def pair_stats(own_p, other, wide):
    count, padded, radii = own_p.shape
    part, lines, _ = other.shape
    flops = 2 * count * part * lines * padded * radii + 12 * count * part * lines * padded
    return pl.pallas_call(
        tile_kernel,
        out_shape=jax.ShapeDtypeStruct((count, part, 8, padded), jnp.float32),
        in_specs=[pl.BlockSpec(memory_space=pltpu.VMEM)] * 3,
        out_specs=pl.BlockSpec(memory_space=pltpu.VMEM),
        scratch_shapes=[pltpu.VMEM((part * lines, padded), jnp.float32)],
        compiler_params=pltpu.CompilerParams(vmem_limit_bytes=48 * 1024 * 1024),
        cost_estimate=pl.CostEstimate(
            flops=flops, transcendentals=count * part * lines * padded, bytes_accessed=2 * 1024 * 1024
        ),
    )(own_p, other.reshape(part * lines, radii), wide)


def pair_tile(own, others, table):
    count, lines, radii = own.shape
    padded = ((lines + 127) // 128) * 128
    own_p = jnp.pad(own, ((0, 0), (0, padded - lines), (0, 0)))
    wide = jnp.broadcast_to(jnp.transpose(table)[:, :, None], (3, lines, 128))
    stats = jnp.concatenate([pair_stats(own_p, other, wide) for other in others], axis=1)
    stats = stats[:, :, :, :lines]
    top = stats[:, :, 0, :]
    peak = jnp.max(top, axis=2, keepdims=True)
    scale = jnp.exp2(top - peak)
    total = jnp.sum(scale * stats[:, :, 1, :], axis=2)
    sums = stats[:, :, 2:5, :] * scale[:, :, None, :]
    rel = jnp.einsum("lp,abql->abpq", table, sums, precision=HIGH)
    rel = rel / total[:, :, None, None]
    return jnp.transpose(rel, (2, 0, 3, 1)).reshape(3 * count, 3 * count)


def butterfly_sum(value, axes, size, bits):
    for bit in bits:
        route = [(i, i ^ bit) for i in range(size)]
        value = value + lax.ppermute(value, axes, route)
    return value


def body(images, partners, counts, start):
    count, lines, radii = images.shape
    width = 3 * count
    slots = partners.shape[1]
    halo = slots // 2
    ncols = lax.axis_size("cols")
    nblk = lax.axis_size("rows")
    size = nblk * ncols
    step = lax.axis_index("cols") + 1
    table = line_table(lines)

    axes = ("rows", "cols")
    route = []
    for i in range(nblk):
        for c in range(ncols):
            route.append((((i + c + 1) % nblk) * ncols + c, i * ncols + c))
    back = [(dst, src) for src, dst in route]
    fetch = lambda v: lax.ppermute(v, axes, route)
    half = count // 2
    first_half = fetch(images[:half])
    second_src, first_half = lax.optimization_barrier((images[half:], first_half))
    others = [first_half, fetch(second_src)]
    packed = jnp.concatenate(
        [partners[0].astype(jnp.float32), counts.astype(jnp.float32), start[0]]
    )
    other_packed = fetch(packed)
    other_partners = other_packed[:slots]
    other_counts = other_packed[slots]
    other_start = other_packed[slots + 1 :]

    tile = pair_tile(images, others, table)

    slot_ids = jnp.arange(slots)
    plus = jnp.any((partners[0] == step + halo - 1) & (slot_ids < counts[0]))
    minus = jnp.any((other_partners == (halo - step).astype(jnp.float32)) & (slot_ids < other_counts))
    col_bits = [1 << b for b in range(ncols.bit_length() - 1)]

    def partial(x_own, x_other):
        forward = jnp.where(plus, jnp.dot(tile, x_other, precision=HIGH), 0.0)
        backward = jnp.where(minus, jnp.dot(tile.T, x_own, precision=HIGH), 0.0)
        return forward + lax.ppermute(backward, axes, back)

    y1 = butterfly_sum(partial(start[0], other_start), axes, size, col_bits)
    z_part = partial(y1, fetch(y1))
    own_square = jnp.where(lax.axis_index("cols") == 0, jnp.sum(y1 * y1), 0.0)
    packet = jnp.concatenate([z_part, own_square[None]])
    gathered = lax.all_to_all(jnp.broadcast_to(packet, (size, width + 1)), axes, 0, 0, tiled=True)
    gathered = gathered.reshape(nblk, ncols, width + 1)
    z_all = gathered[:, 0, :width]
    for c in range(1, ncols):
        z_all = z_all + gathered[:, c, :width]
    sum_y1 = jnp.sum(gathered[:, :, width])
    sum_z = jnp.sum(z_all * z_all)
    z = lax.dynamic_index_in_dim(z_all, lax.axis_index("rows"), 0, keepdims=False)
    entries = float(width * nblk)
    s1 = jnp.sqrt(sum_y1 / entries + norm_eps)
    first_vec = y1 / s1
    second_raw = z / s1
    s2 = jnp.sqrt(sum_z / (s1 * s1) / entries + norm_eps)
    return (first_vec[None, :], (second_raw / s2)[None, :])


def solution(mesh):
    in_specs = (P("rows", None, None), P("rows", None), P("rows"), P("rows", None))
    out_specs = (P("rows", None), P("rows", None))
    return jax.shard_map(body, mesh=mesh, in_specs=in_specs, out_specs=out_specs, check_vma=False)
```

```python
import math

import jax
import jax.numpy as jnp
from jax import lax
from jax.experimental import pallas as pl
from jax.experimental.pallas import tpu as pltpu
from jax.sharding import PartitionSpec as P

score_gain = 0.4
norm_eps = 1e-06
HIGH = lax.Precision.HIGHEST
LOG2E = 1.4426950408889634


def line_table(lines):
    angle = 2.0 * math.pi * jnp.arange(lines).astype(jnp.float32) / lines
    return jnp.stack([jnp.cos(angle), jnp.sin(angle), jnp.cos(2.0 * angle)], axis=1)


def tile_kernel(a_ref, b_ref, w_ref, o_ref, s_ref):
    n = a_ref.shape[0]
    lines = w_ref.shape[1]
    nb = b_ref.shape[0] // lines
    width = a_ref.shape[1]
    groups = width // 128
    strips = lines // 8

    def per_image(a, carry):
        s_ref[...] = (
            lax.dot_general(
                b_ref[...], a_ref[a], (((1,), (1,)), ((), ())), preferred_element_type=jnp.float32
            )
            * (score_gain * LOG2E)
        )

        def per_partner(b, carry2):
            base = b * lines

            def col_max(r, m):
                start = pl.multiple_of(base + r * 8, 8)
                return jnp.maximum(m, s_ref[pl.ds(start, 8), :])

            m8 = lax.fori_loop(0, strips, col_max, jnp.full((8, width), -jnp.inf, jnp.float32), unroll=True)
            top = jnp.max(m8, axis=0, keepdims=True)
            top8 = jnp.broadcast_to(top, (8, width))

            def accumulate(r, acc):
                start = pl.multiple_of(base + r * 8, 8)
                e = jnp.exp2(s_ref[pl.ds(start, 8), :] - top8)
                row = pl.multiple_of(r * 8, 8)
                out = [acc[0] + e]
                for q in range(3):
                    wq = w_ref[q, pl.ds(row, 8), :]
                    wide = jnp.concatenate([wq] * groups, axis=1)
                    out.append(acc[q + 1] + e * wide)
                return tuple(out)

            zero = jnp.zeros((8, width), jnp.float32)
            acc = lax.fori_loop(0, strips, accumulate, (zero, zero, zero, zero), unroll=True)
            o_ref[a, b, 0:1, :] = top
            for j in range(4):
                o_ref[a, b, j + 1 : j + 2, :] = jnp.sum(acc[j], axis=0, keepdims=True)
            return carry2

        lax.fori_loop(0, nb, per_partner, 0)
        return carry

    lax.fori_loop(0, n, per_image, 0)


def pair_stats(own_p, other, wide):
    count, padded, radii = own_p.shape
    part, lines, _ = other.shape
    flops = 2 * count * part * lines * padded * radii + 12 * count * part * lines * padded
    return pl.pallas_call(
        tile_kernel,
        out_shape=jax.ShapeDtypeStruct((count, part, 8, padded), jnp.float32),
        in_specs=[pl.BlockSpec(memory_space=pltpu.VMEM)] * 3,
        out_specs=pl.BlockSpec(memory_space=pltpu.VMEM),
        scratch_shapes=[pltpu.VMEM((part * lines, padded), jnp.float32)],
        compiler_params=pltpu.CompilerParams(vmem_limit_bytes=48 * 1024 * 1024),
        cost_estimate=pl.CostEstimate(
            flops=flops, transcendentals=count * part * lines * padded, bytes_accessed=2 * 1024 * 1024
        ),
    )(own_p, other.reshape(part * lines, radii), wide)


def pair_tile(own, others, table):
    count, lines, radii = own.shape
    padded = ((lines + 127) // 128) * 128
    own_p = jnp.pad(own, ((0, 0), (0, padded - lines), (0, 0)))
    wide = jnp.broadcast_to(jnp.transpose(table)[:, :, None], (3, lines, 128))
    stats = jnp.concatenate([pair_stats(own_p, other, wide) for other in others], axis=1)
    stats = stats[:, :, :, :lines]
    top = stats[:, :, 0, :]
    peak = jnp.max(top, axis=2, keepdims=True)
    scale = jnp.exp2(top - peak)
    total = jnp.sum(scale * stats[:, :, 1, :], axis=2)
    sums = stats[:, :, 2:5, :] * scale[:, :, None, :]
    rel = jnp.sum(jnp.transpose(table)[None, None, :, None, :] * sums[:, :, None, :, :], axis=-1)
    rel = rel / total[:, :, None, None]
    return jnp.transpose(rel, (2, 0, 3, 1)).reshape(3 * count, 3 * count)


def butterfly_sum(value, axes, size, bits):
    for bit in bits:
        route = [(i, i ^ bit) for i in range(size)]
        value = value + lax.ppermute(value, axes, route)
    return value


def body(images, partners, counts, start):
    count, lines, radii = images.shape
    width = 3 * count
    slots = partners.shape[1]
    halo = slots // 2
    ncols = lax.axis_size("cols")
    nblk = lax.axis_size("rows")
    size = nblk * ncols
    step = lax.axis_index("cols") + 1
    table = line_table(lines)

    axes = ("rows", "cols")
    route = []
    for i in range(nblk):
        for c in range(ncols):
            route.append((((i + c + 1) % nblk) * ncols + c, i * ncols + c))
    back = [(dst, src) for src, dst in route]
    fetch = lambda v: lax.ppermute(v, axes, route)
    half = count // 2
    first_half = fetch(images[:half])
    second_src, first_half = lax.optimization_barrier((images[half:], first_half))
    others = [first_half, fetch(second_src)]
    slot_ids = jnp.arange(slots)
    plus = jnp.any((partners[0] == step + halo - 1) & (slot_ids < counts[0]))
    own_minus = jnp.any((partners[0] == halo - step) & (slot_ids < counts[0]))
    packed = jnp.concatenate([start[0], own_minus.astype(jnp.float32)[None]])
    other_packed = fetch(packed)
    minus = other_packed[width] > 0.5
    other_start = other_packed[:width]

    tile = pair_tile(images, others, table)

    col_bits = [1 << b for b in range(ncols.bit_length() - 1)]

    def partial(x_own, x_other):
        forward = jnp.where(plus, jnp.dot(tile, x_other, precision=HIGH), 0.0)
        backward = jnp.where(minus, jnp.dot(tile.T, x_own, precision=HIGH), 0.0)
        return forward + lax.ppermute(backward, axes, back)

    y1 = butterfly_sum(partial(start[0], other_start), axes, size, col_bits)
    z_part = partial(y1, fetch(y1))
    own_square = jnp.where(lax.axis_index("cols") == 0, jnp.sum(y1 * y1), 0.0)
    packet = jnp.concatenate([z_part, own_square[None]])
    gathered = lax.all_to_all(jnp.broadcast_to(packet, (size, width + 1)), axes, 0, 0, tiled=True)
    gathered = gathered.reshape(nblk, ncols, width + 1)
    z_all = gathered[:, 0, :width]
    for c in range(1, ncols):
        z_all = z_all + gathered[:, c, :width]
    sum_y1 = jnp.sum(gathered[:, :, width])
    sum_z = jnp.sum(z_all * z_all)
    z = lax.dynamic_index_in_dim(z_all, lax.axis_index("rows"), 0, keepdims=False)
    entries = float(width * nblk)
    s1 = jnp.sqrt(sum_y1 / entries + norm_eps)
    first_vec = y1 / s1
    second_raw = z / s1
    s2 = jnp.sqrt(sum_z / (s1 * s1) / entries + norm_eps)
    return (first_vec[None, :], (second_raw / s2)[None, :])


def solution(mesh):
    in_specs = (P("rows", None, None), P("rows", None), P("rows"), P("rows", None))
    out_specs = (P("rows", None), P("rows", None))
    return jax.shard_map(body, mesh=mesh, in_specs=in_specs, out_specs=out_specs, check_vma=False)
```

```python
import math

import jax
import jax.numpy as jnp
from jax import lax
from jax.experimental import pallas as pl
from jax.experimental.pallas import tpu as pltpu
from jax.sharding import PartitionSpec as P

score_gain = 0.4
norm_eps = 1e-06
HIGH = lax.Precision.HIGHEST
LOG2E = 1.4426950408889634


def line_table(lines):
    angle = 2.0 * math.pi * jnp.arange(lines).astype(jnp.float32) / lines
    return jnp.stack([jnp.cos(angle), jnp.sin(angle), jnp.cos(2.0 * angle)], axis=1)


def tile_kernel(a_ref, b_ref, w_ref, o_ref, s_ref):
    n = a_ref.shape[0]
    lines = w_ref.shape[1]
    nb = b_ref.shape[0] // lines
    width = a_ref.shape[1]
    groups = width // 128
    strips = lines // 8

    def per_image(a, carry):
        s_ref[...] = (
            lax.dot_general(
                b_ref[...], a_ref[a], (((1,), (1,)), ((), ())), preferred_element_type=jnp.float32
            )
            * (score_gain * LOG2E)
        )

        def per_partner(b, carry2):
            base = b * lines

            def col_max(r, m):
                start = pl.multiple_of(base + r * 8, 8)
                return jnp.maximum(m, s_ref[pl.ds(start, 8), :])

            m8 = lax.fori_loop(0, strips, col_max, jnp.full((8, width), -jnp.inf, jnp.float32), unroll=True)
            top = jnp.max(m8, axis=0, keepdims=True)
            top8 = jnp.broadcast_to(top, (8, width))

            def accumulate(r, acc):
                start = pl.multiple_of(base + r * 8, 8)
                e = jnp.exp2(s_ref[pl.ds(start, 8), :] - top8)
                row = pl.multiple_of(r * 8, 8)
                out = [acc[0] + e]
                for q in range(3):
                    wq = w_ref[q, pl.ds(row, 8), :]
                    wide = jnp.concatenate([wq] * groups, axis=1)
                    out.append(acc[q + 1] + e * wide)
                return tuple(out)

            zero = jnp.zeros((8, width), jnp.float32)
            acc = lax.fori_loop(0, strips, accumulate, (zero, zero, zero, zero), unroll=True)
            o_ref[a, b, 0:1, :] = top
            for j in range(4):
                o_ref[a, b, j + 1 : j + 2, :] = jnp.sum(acc[j], axis=0, keepdims=True)
            return carry2

        lax.fori_loop(0, nb, per_partner, 0)
        return carry

    lax.fori_loop(0, n, per_image, 0)


def pair_stats(own_p, other, wide):
    count, padded, radii = own_p.shape
    part, lines, _ = other.shape
    flops = 2 * count * part * lines * padded * radii + 12 * count * part * lines * padded
    return pl.pallas_call(
        tile_kernel,
        out_shape=jax.ShapeDtypeStruct((count, part, 8, padded), jnp.float32),
        in_specs=[pl.BlockSpec(memory_space=pltpu.VMEM)] * 3,
        out_specs=pl.BlockSpec(memory_space=pltpu.VMEM),
        scratch_shapes=[pltpu.VMEM((part * lines, padded), jnp.float32)],
        compiler_params=pltpu.CompilerParams(vmem_limit_bytes=48 * 1024 * 1024),
        cost_estimate=pl.CostEstimate(
            flops=flops, transcendentals=count * part * lines * padded, bytes_accessed=2 * 1024 * 1024
        ),
    )(own_p, other.reshape(part * lines, radii), wide)


def pair_tile(own, others, table):
    count, lines, radii = own.shape
    padded = ((lines + 127) // 128) * 128
    own_p = jnp.pad(own, ((0, 0), (0, padded - lines), (0, 0)))
    wide = jnp.broadcast_to(jnp.transpose(table)[:, :, None], (3, lines, 128))
    stats = jnp.concatenate([pair_stats(own_p, other, wide) for other in others], axis=1)
    stats = stats[:, :, :, :lines]
    top = stats[:, :, 0, :]
    peak = jnp.max(top, axis=2, keepdims=True)
    scale = jnp.exp2(top - peak)
    total = jnp.sum(scale * stats[:, :, 1, :], axis=2)
    sums = stats[:, :, 2:5, :] * scale[:, :, None, :]
    rel = jnp.sum(jnp.transpose(table)[None, None, :, None, :] * sums[:, :, None, :, :], axis=-1)
    rel = rel / total[:, :, None, None]
    return jnp.transpose(rel, (2, 0, 3, 1)).reshape(3 * count, 3 * count)


def butterfly_sum(value, axes, size, bits):
    for bit in bits:
        route = [(i, i ^ bit) for i in range(size)]
        value = value + lax.ppermute(value, axes, route)
    return value


def body(images, partners, counts, start):
    count, lines, radii = images.shape
    width = 3 * count
    slots = partners.shape[1]
    halo = slots // 2
    ncols = lax.axis_size("cols")
    nblk = lax.axis_size("rows")
    size = nblk * ncols
    step = lax.axis_index("cols") + 1
    table = line_table(lines)

    axes = ("rows", "cols")
    route = []
    for i in range(nblk):
        for c in range(ncols):
            route.append((((i + c + 1) % nblk) * ncols + c, i * ncols + c))
    back = [(dst, src) for src, dst in route]
    fetch = lambda v: lax.ppermute(v, axes, route)
    half = count // 2
    first_half = fetch(images[:half])
    second_src, first_half = lax.optimization_barrier((images[half:], first_half))
    others = [first_half, fetch(second_src)]
    slot_ids = jnp.arange(slots)
    plus = jnp.any((partners[0] == step + halo - 1) & (slot_ids < counts[0]))
    own_minus = jnp.any((partners[0] == halo - step) & (slot_ids < counts[0]))
    packed = jnp.concatenate([start[0], own_minus.astype(jnp.float32)[None]])
    other_packed = fetch(packed)
    minus = other_packed[width] > 0.5
    other_start = other_packed[:width]

    tile = pair_tile(images, others, table)

    col_bits = [1 << b for b in range(ncols.bit_length() - 1)]

    forward = jnp.where(plus, jnp.dot(tile, other_start, precision=HIGH), 0.0)
    backward = jnp.where(minus, jnp.dot(tile.T, start[0], precision=HIGH), 0.0)
    sent = jnp.concatenate([backward, tile.reshape(width * width), plus.astype(jnp.float32)[None]])
    got = lax.ppermute(sent, axes, back)
    y1 = butterfly_sum(forward + got[:width], axes, size, col_bits)
    tile_below = got[width : width + width * width].reshape(width, width)
    plus_below = got[width + width * width] > 0.5
    up = jnp.where(minus, jnp.dot(tile.T, y1, precision=HIGH), 0.0)
    down = jnp.where(plus_below, jnp.dot(tile_below, y1, precision=HIGH), 0.0)
    own_square = jnp.where(lax.axis_index("cols") == 0, jnp.sum(y1 * y1), 0.0)
    packet = jnp.concatenate([up, down, own_square[None]])
    gathered = lax.all_to_all(jnp.broadcast_to(packet, (size, 2 * width + 1)), axes, 0, 0, tiled=True)
    gathered = gathered.reshape(nblk, ncols, 2 * width + 1)
    z_all = jnp.roll(gathered[:, 0, :width], 1, axis=0)
    for c in range(1, ncols):
        z_all = z_all + jnp.roll(gathered[:, c, :width], c + 1, axis=0)
    for c in range(ncols):
        z_all = z_all + jnp.roll(gathered[:, c, width : 2 * width], -(c + 1), axis=0)
    sum_y1 = jnp.sum(gathered[:, :, 2 * width])
    sum_z = jnp.sum(z_all * z_all)
    z = lax.dynamic_index_in_dim(z_all, lax.axis_index("rows"), 0, keepdims=False)
    entries = float(width * nblk)
    s1 = jnp.sqrt(sum_y1 / entries + norm_eps)
    first_vec = y1 / s1
    second_raw = z / s1
    s2 = jnp.sqrt(sum_z / (s1 * s1) / entries + norm_eps)
    return (first_vec[None, :], (second_raw / s2)[None, :])


def solution(mesh):
    in_specs = (P("rows", None, None), P("rows", None), P("rows"), P("rows", None))
    out_specs = (P("rows", None), P("rows", None))
    return jax.shard_map(body, mesh=mesh, in_specs=in_specs, out_specs=out_specs, check_vma=False)
```

```python
import math

import jax
import jax.numpy as jnp
from jax import lax
from jax.experimental import pallas as pl
from jax.experimental.pallas import tpu as pltpu
from jax.sharding import PartitionSpec as P

score_gain = 0.4
norm_eps = 1e-06
HIGH = lax.Precision.HIGHEST
LOG2E = 1.4426950408889634


def line_table(lines):
    angle = 2.0 * math.pi * jnp.arange(lines).astype(jnp.float32) / lines
    return jnp.stack([jnp.cos(angle), jnp.sin(angle), jnp.cos(2.0 * angle)], axis=1)


def tile_kernel(a_ref, b_ref, w_ref, o_ref, s_ref):
    n = a_ref.shape[0]
    lines = w_ref.shape[1]
    nb = b_ref.shape[0] // lines
    width = a_ref.shape[1]
    groups = width // 128
    strips = lines // 8

    def per_image(a, carry):
        s_ref[...] = (
            lax.dot_general(
                b_ref[...], a_ref[a], (((1,), (1,)), ((), ())), preferred_element_type=jnp.float32
            )
            * (score_gain * LOG2E)
        )

        def per_partner(b, carry2):
            base = b * lines

            def col_max(r, m):
                start = pl.multiple_of(base + r * 8, 8)
                return jnp.maximum(m, s_ref[pl.ds(start, 8), :])

            m8 = lax.fori_loop(0, strips, col_max, jnp.full((8, width), -jnp.inf, jnp.float32), unroll=True)
            top = jnp.max(m8, axis=0, keepdims=True)
            top8 = jnp.broadcast_to(top, (8, width))

            def accumulate(r, acc):
                start = pl.multiple_of(base + r * 8, 8)
                e = jnp.exp2(s_ref[pl.ds(start, 8), :] - top8)
                row = pl.multiple_of(r * 8, 8)
                out = [acc[0] + e]
                for q in range(3):
                    wq = w_ref[q, pl.ds(row, 8), :]
                    wide = jnp.concatenate([wq] * groups, axis=1)
                    out.append(acc[q + 1] + e * wide)
                return tuple(out)

            zero = jnp.zeros((8, width), jnp.float32)
            acc = lax.fori_loop(0, strips, accumulate, (zero, zero, zero, zero), unroll=True)
            o_ref[a, b, 0:1, :] = top
            for j in range(4):
                o_ref[a, b, j + 1 : j + 2, :] = jnp.sum(acc[j], axis=0, keepdims=True)
            return carry2

        lax.fori_loop(0, nb, per_partner, 0)
        return carry

    lax.fori_loop(0, n, per_image, 0)


def pair_stats(own_p, other, wide):
    count, padded, radii = own_p.shape
    part, lines, _ = other.shape
    flops = 2 * count * part * lines * padded * radii + 12 * count * part * lines * padded
    return pl.pallas_call(
        tile_kernel,
        out_shape=jax.ShapeDtypeStruct((count, part, 8, padded), jnp.float32),
        in_specs=[pl.BlockSpec(memory_space=pltpu.VMEM)] * 3,
        out_specs=pl.BlockSpec(memory_space=pltpu.VMEM),
        scratch_shapes=[pltpu.VMEM((part * lines, padded), jnp.float32)],
        compiler_params=pltpu.CompilerParams(vmem_limit_bytes=48 * 1024 * 1024),
        cost_estimate=pl.CostEstimate(
            flops=flops, transcendentals=count * part * lines * padded, bytes_accessed=2 * 1024 * 1024
        ),
    )(own_p, other.reshape(part * lines, radii), wide)


def pair_tile(own, others, table):
    count, lines, radii = own.shape
    padded = ((lines + 127) // 128) * 128
    own_p = jnp.pad(own, ((0, 0), (0, padded - lines), (0, 0)))
    wide = jnp.broadcast_to(jnp.transpose(table)[:, :, None], (3, lines, 128))
    stats = jnp.concatenate([pair_stats(own_p, other, wide) for other in others], axis=1)
    stats = stats[:, :, :, :lines]
    top = stats[:, :, 0, :]
    peak = jnp.max(top, axis=2, keepdims=True)
    scale = jnp.exp2(top - peak)
    total = jnp.sum(scale * stats[:, :, 1, :], axis=2)
    sums = stats[:, :, 2:5, :] * scale[:, :, None, :]
    rel = jnp.sum(jnp.transpose(table)[None, None, :, None, :] * sums[:, :, None, :, :], axis=-1)
    rel = rel / total[:, :, None, None]
    return jnp.transpose(rel, (2, 0, 3, 1)).reshape(3 * count, 3 * count)


def butterfly_sum(value, axes, size, bits):
    for bit in bits:
        route = [(i, i ^ bit) for i in range(size)]
        value = value + lax.ppermute(value, axes, route)
    return value


def body(images, partners, counts, start):
    count, lines, radii = images.shape
    width = 3 * count
    slots = partners.shape[1]
    halo = slots // 2
    ncols = lax.axis_size("cols")
    nblk = lax.axis_size("rows")
    size = nblk * ncols
    step = lax.axis_index("cols") + 1
    table = line_table(lines)

    axes = ("rows", "cols")
    route = []
    for i in range(nblk):
        for c in range(ncols):
            route.append((((i + c + 1) % nblk) * ncols + c, i * ncols + c))
    back = [(dst, src) for src, dst in route]
    fetch = lambda v: lax.ppermute(v, axes, route)
    others = [fetch(images)]
    slot_ids = jnp.arange(slots)
    plus = jnp.any((partners[0] == step + halo - 1) & (slot_ids < counts[0]))
    own_minus = jnp.any((partners[0] == halo - step) & (slot_ids < counts[0]))
    packed = jnp.concatenate([start[0], own_minus.astype(jnp.float32)[None]])
    other_packed = fetch(packed)
    minus = other_packed[width] > 0.5
    other_start = other_packed[:width]

    tile = pair_tile(images, others, table)

    col_bits = [1 << b for b in range(ncols.bit_length() - 1)]

    forward = jnp.where(plus, jnp.dot(tile, other_start, precision=HIGH), 0.0)
    backward = jnp.where(minus, jnp.dot(tile.T, start[0], precision=HIGH), 0.0)
    sent = jnp.concatenate([backward, tile.reshape(width * width), plus.astype(jnp.float32)[None]])
    got = lax.ppermute(sent, axes, back)
    y1 = butterfly_sum(forward + got[:width], axes, size, col_bits)
    tile_below = got[width : width + width * width].reshape(width, width)
    plus_below = got[width + width * width] > 0.5
    up = jnp.where(minus, jnp.dot(tile.T, y1, precision=HIGH), 0.0)
    down = jnp.where(plus_below, jnp.dot(tile_below, y1, precision=HIGH), 0.0)
    own_square = jnp.where(lax.axis_index("cols") == 0, jnp.sum(y1 * y1), 0.0)
    packet = jnp.concatenate([up, down, own_square[None]])
    gathered = lax.all_to_all(jnp.broadcast_to(packet, (size, 2 * width + 1)), axes, 0, 0, tiled=True)
    gathered = gathered.reshape(nblk, ncols, 2 * width + 1)
    z_all = jnp.roll(gathered[:, 0, :width], 1, axis=0)
    for c in range(1, ncols):
        z_all = z_all + jnp.roll(gathered[:, c, :width], c + 1, axis=0)
    for c in range(ncols):
        z_all = z_all + jnp.roll(gathered[:, c, width : 2 * width], -(c + 1), axis=0)
    sum_y1 = jnp.sum(gathered[:, :, 2 * width])
    sum_z = jnp.sum(z_all * z_all)
    z = lax.dynamic_index_in_dim(z_all, lax.axis_index("rows"), 0, keepdims=False)
    entries = float(width * nblk)
    s1 = jnp.sqrt(sum_y1 / entries + norm_eps)
    first_vec = y1 / s1
    second_raw = z / s1
    s2 = jnp.sqrt(sum_z / (s1 * s1) / entries + norm_eps)
    return (first_vec[None, :], (second_raw / s2)[None, :])


def solution(mesh):
    in_specs = (P("rows", None, None), P("rows", None), P("rows"), P("rows", None))
    out_specs = (P("rows", None), P("rows", None))
    return jax.shard_map(body, mesh=mesh, in_specs=in_specs, out_specs=out_specs, check_vma=False)
```

```python
import math

import jax
import jax.numpy as jnp
from jax import lax
from jax.experimental import pallas as pl
from jax.experimental.pallas import tpu as pltpu
from jax.sharding import PartitionSpec as P

score_gain = 0.4
norm_eps = 1e-06
HIGH = lax.Precision.HIGHEST
LOG2E = 1.4426950408889634


def line_table(lines):
    angle = 2.0 * math.pi * jnp.arange(lines).astype(jnp.float32) / lines
    return jnp.stack([jnp.cos(angle), jnp.sin(angle), jnp.cos(2.0 * angle)], axis=1)


def tile_kernel(a_ref, b_ref, w_ref, o_ref, s_ref):
    n = a_ref.shape[0]
    lines = w_ref.shape[1]
    nb = b_ref.shape[0] // lines
    width = a_ref.shape[1]
    groups = width // 128
    strips = lines // 8

    def per_image(a, carry):
        s_ref[...] = (
            lax.dot_general(
                b_ref[...], a_ref[a], (((1,), (1,)), ((), ())), preferred_element_type=jnp.float32
            )
            * (score_gain * LOG2E)
        )

        def per_partner(b, carry2):
            base = b * lines

            def col_max(r, m):
                start = pl.multiple_of(base + r * 8, 8)
                return jnp.maximum(m, s_ref[pl.ds(start, 8), :])

            m8 = lax.fori_loop(0, strips, col_max, jnp.full((8, width), -jnp.inf, jnp.float32), unroll=True)
            top = jnp.max(m8, axis=0, keepdims=True)
            top8 = jnp.broadcast_to(top, (8, width))

            def accumulate(r, acc):
                start = pl.multiple_of(base + r * 8, 8)
                e = jnp.exp2(s_ref[pl.ds(start, 8), :] - top8)
                row = pl.multiple_of(r * 8, 8)
                out = [acc[0] + e]
                for q in range(3):
                    wq = w_ref[q, pl.ds(row, 8), :]
                    wide = jnp.concatenate([wq] * groups, axis=1)
                    out.append(acc[q + 1] + e * wide)
                return tuple(out)

            zero = jnp.zeros((8, width), jnp.float32)
            acc = lax.fori_loop(0, strips, accumulate, (zero, zero, zero, zero), unroll=True)
            o_ref[a, b, 0:1, :] = top
            for j in range(4):
                o_ref[a, b, j + 1 : j + 2, :] = jnp.sum(acc[j], axis=0, keepdims=True)
            return carry2

        lax.fori_loop(0, nb, per_partner, 0)
        return carry

    lax.fori_loop(0, n, per_image, 0)


def pair_stats(own_p, other, wide):
    count, padded, radii = own_p.shape
    part, lines, _ = other.shape
    flops = 2 * count * part * lines * padded * radii + 12 * count * part * lines * padded
    return pl.pallas_call(
        tile_kernel,
        out_shape=jax.ShapeDtypeStruct((count, part, 8, padded), jnp.float32),
        in_specs=[pl.BlockSpec(memory_space=pltpu.VMEM)] * 3,
        out_specs=pl.BlockSpec(memory_space=pltpu.VMEM),
        scratch_shapes=[pltpu.VMEM((part * lines, padded), jnp.float32)],
        compiler_params=pltpu.CompilerParams(vmem_limit_bytes=48 * 1024 * 1024),
        cost_estimate=pl.CostEstimate(
            flops=flops, transcendentals=count * part * lines * padded, bytes_accessed=2 * 1024 * 1024
        ),
    )(own_p, other.reshape(part * lines, radii), wide)


def pair_tile(own, others, table):
    count, lines, radii = own.shape
    padded = ((lines + 127) // 128) * 128
    own_p = jnp.pad(own, ((0, 0), (0, padded - lines), (0, 0)))
    wide = jnp.broadcast_to(jnp.transpose(table)[:, :, None], (3, lines, 128))
    stats = jnp.concatenate([pair_stats(own_p, other, wide) for other in others], axis=1)
    stats = stats[:, :, :, :lines]
    top = stats[:, :, 0, :]
    peak = jnp.max(top, axis=2, keepdims=True)
    scale = jnp.exp2(top - peak)
    total = jnp.sum(scale * stats[:, :, 1, :], axis=2)
    sums = stats[:, :, 2:5, :] * scale[:, :, None, :]
    rel = jnp.sum(jnp.transpose(table)[None, None, :, None, :] * sums[:, :, None, :, :], axis=-1)
    rel = rel / total[:, :, None, None]
    return jnp.transpose(rel, (2, 0, 3, 1)).reshape(3 * count, 3 * count)


def butterfly_sum(value, axes, size, bits):
    for bit in bits:
        route = [(i, i ^ bit) for i in range(size)]
        value = value + lax.ppermute(value, axes, route)
    return value


def body(images, partners, counts, start):
    count, lines, radii = images.shape
    width = 3 * count
    slots = partners.shape[1]
    halo = slots // 2
    ncols = lax.axis_size("cols")
    nblk = lax.axis_size("rows")
    size = nblk * ncols
    step = lax.axis_index("cols") + 1
    table = line_table(lines)

    axes = ("rows", "cols")
    route = []
    for i in range(nblk):
        for c in range(ncols):
            route.append((((i + c + 1) % nblk) * ncols + c, i * ncols + c))
    back = [(dst, src) for src, dst in route]
    fetch = lambda v: lax.ppermute(v, axes, route)
    half = count // 2
    first_half = fetch(images[:half])
    second_src, first_half = lax.optimization_barrier((images[half:], first_half))
    others = [first_half, fetch(second_src)]
    slot_ids = jnp.arange(slots)
    plus = jnp.any((partners[0] == step + halo - 1) & (slot_ids < counts[0]))
    own_minus = jnp.any((partners[0] == halo - step) & (slot_ids < counts[0]))
    packed = jnp.concatenate([start[0], own_minus.astype(jnp.float32)[None]])
    other_packed = fetch(packed)
    minus = other_packed[width] > 0.5
    other_start = other_packed[:width]

    tile = pair_tile(images, others, table)

    col_bits = [1 << b for b in range(ncols.bit_length() - 1)]

    forward = jnp.where(plus, jnp.dot(tile, other_start, precision=HIGH), 0.0)
    backward = jnp.where(minus, jnp.dot(tile.T, start[0], precision=HIGH), 0.0)
    sent = jnp.concatenate([backward, tile.reshape(width * width), plus.astype(jnp.float32)[None]])
    got = lax.ppermute(sent, axes, back)
    parts = lax.all_to_all(jnp.broadcast_to(forward + got[:width], (ncols, width)), "cols", 0, 0, tiled=True)
    y1 = parts[0]
    for c in range(1, ncols):
        y1 = y1 + parts[c]
    tile_below = got[width : width + width * width].reshape(width, width)
    plus_below = got[width + width * width] > 0.5
    up = jnp.where(minus, jnp.dot(tile.T, y1, precision=HIGH), 0.0)
    down = jnp.where(plus_below, jnp.dot(tile_below, y1, precision=HIGH), 0.0)
    own_square = jnp.where(lax.axis_index("cols") == 0, jnp.sum(y1 * y1), 0.0)
    packet = jnp.concatenate([up, down, own_square[None]])
    gathered = lax.all_to_all(jnp.broadcast_to(packet, (size, 2 * width + 1)), axes, 0, 0, tiled=True)
    gathered = gathered.reshape(nblk, ncols, 2 * width + 1)
    z_all = jnp.roll(gathered[:, 0, :width], 1, axis=0)
    for c in range(1, ncols):
        z_all = z_all + jnp.roll(gathered[:, c, :width], c + 1, axis=0)
    for c in range(ncols):
        z_all = z_all + jnp.roll(gathered[:, c, width : 2 * width], -(c + 1), axis=0)
    sum_y1 = jnp.sum(gathered[:, :, 2 * width])
    sum_z = jnp.sum(z_all * z_all)
    z = lax.dynamic_index_in_dim(z_all, lax.axis_index("rows"), 0, keepdims=False)
    entries = float(width * nblk)
    s1 = jnp.sqrt(sum_y1 / entries + norm_eps)
    first_vec = y1 / s1
    second_raw = z / s1
    s2 = jnp.sqrt(sum_z / (s1 * s1) / entries + norm_eps)
    return (first_vec[None, :], (second_raw / s2)[None, :])


def solution(mesh):
    in_specs = (P("rows", None, None), P("rows", None), P("rows"), P("rows", None))
    out_specs = (P("rows", None), P("rows", None))
    return jax.shard_map(body, mesh=mesh, in_specs=in_specs, out_specs=out_specs, check_vma=False)
```

```python
import math

import jax
import jax.numpy as jnp
from jax import lax
from jax.experimental import pallas as pl
from jax.experimental.pallas import tpu as pltpu
from jax.sharding import PartitionSpec as P

score_gain = 0.4
norm_eps = 1e-06
HIGH = lax.Precision.HIGHEST
LOG2E = 1.4426950408889634


def line_table(lines):
    angle = 2.0 * math.pi * jnp.arange(lines).astype(jnp.float32) / lines
    return jnp.stack([jnp.cos(angle), jnp.sin(angle), jnp.cos(2.0 * angle)], axis=1)


def tile_kernel(a_ref, b_ref, w_ref, o_ref, s_ref):
    n = a_ref.shape[0]
    lines = w_ref.shape[1]
    nb = b_ref.shape[0] // lines
    width = a_ref.shape[1]
    groups = width // 128
    strips = lines // 8

    def per_image(a, carry):
        s_ref[...] = (
            lax.dot_general(
                b_ref[...], a_ref[a], (((1,), (1,)), ((), ())), preferred_element_type=jnp.float32
            )
            * (score_gain * LOG2E)
        )

        def per_partner(b, carry2):
            base = b * lines

            def col_max(r, m):
                start = pl.multiple_of(base + r * 8, 8)
                return jnp.maximum(m, s_ref[pl.ds(start, 8), :])

            m8 = lax.fori_loop(0, strips, col_max, jnp.full((8, width), -jnp.inf, jnp.float32), unroll=True)
            top = jnp.max(m8, axis=0, keepdims=True)
            top8 = jnp.broadcast_to(top, (8, width))

            def accumulate(r, acc):
                start = pl.multiple_of(base + r * 8, 8)
                e = jnp.exp2(s_ref[pl.ds(start, 8), :] - top8)
                row = pl.multiple_of(r * 8, 8)
                out = [acc[0] + e]
                for q in range(3):
                    wq = w_ref[q, pl.ds(row, 8), :]
                    wide = jnp.concatenate([wq] * groups, axis=1)
                    out.append(acc[q + 1] + e * wide)
                return tuple(out)

            zero = jnp.zeros((8, width), jnp.float32)
            acc = lax.fori_loop(0, strips, accumulate, (zero, zero, zero, zero), unroll=True)
            o_ref[a, b, 0:1, :] = top
            for j in range(4):
                o_ref[a, b, j + 1 : j + 2, :] = jnp.sum(acc[j], axis=0, keepdims=True)
            return carry2

        lax.fori_loop(0, nb, per_partner, 0)
        return carry

    lax.fori_loop(0, n, per_image, 0)


def pair_stats(own_p, other, wide):
    count, padded, radii = own_p.shape
    part, lines, _ = other.shape
    flops = 2 * count * part * lines * padded * radii + 12 * count * part * lines * padded
    return pl.pallas_call(
        tile_kernel,
        out_shape=jax.ShapeDtypeStruct((count, part, 8, padded), jnp.float32),
        in_specs=[pl.BlockSpec(memory_space=pltpu.VMEM)] * 3,
        out_specs=pl.BlockSpec(memory_space=pltpu.VMEM),
        scratch_shapes=[pltpu.VMEM((part * lines, padded), jnp.float32)],
        compiler_params=pltpu.CompilerParams(vmem_limit_bytes=48 * 1024 * 1024),
        cost_estimate=pl.CostEstimate(
            flops=flops, transcendentals=count * part * lines * padded, bytes_accessed=2 * 1024 * 1024
        ),
    )(own_p, other.reshape(part * lines, radii), wide)


def pair_tile(own, others, table):
    count, lines, radii = own.shape
    padded = ((lines + 127) // 128) * 128
    own_p = jnp.pad(own, ((0, 0), (0, padded - lines), (0, 0)))
    wide = jnp.broadcast_to(jnp.transpose(table)[:, :, None], (3, lines, 128))
    stats = jnp.concatenate([pair_stats(own_p, other, wide) for other in others], axis=1)
    stats = stats[:, :, :, :lines]
    top = stats[:, :, 0, :]
    peak = jnp.max(top, axis=2, keepdims=True)
    scale = jnp.exp2(top - peak)
    total = jnp.sum(scale * stats[:, :, 1, :], axis=2)
    sums = stats[:, :, 2:5, :] * scale[:, :, None, :]
    rel = jnp.sum(jnp.transpose(table)[None, None, :, None, :] * sums[:, :, None, :, :], axis=-1)
    rel = rel / total[:, :, None, None]
    return jnp.transpose(rel, (2, 0, 3, 1)).reshape(3 * count, 3 * count)


def butterfly_sum(value, axes, size, bits):
    for bit in bits:
        route = [(i, i ^ bit) for i in range(size)]
        value = value + lax.ppermute(value, axes, route)
    return value


def body(images, partners, counts, start):
    count, lines, radii = images.shape
    width = 3 * count
    slots = partners.shape[1]
    halo = slots // 2
    ncols = lax.axis_size("cols")
    nblk = lax.axis_size("rows")
    size = nblk * ncols
    step = lax.axis_index("cols") + 1
    table = line_table(lines)

    axes = ("rows", "cols")
    route = []
    for i in range(nblk):
        for c in range(ncols):
            route.append((((i + c + 1) % nblk) * ncols + c, i * ncols + c))
    back = [(dst, src) for src, dst in route]
    fetch = lambda v: lax.ppermute(v, axes, route)
    half = count // 2
    first_half = fetch(images[:half])
    second_src, first_half = lax.optimization_barrier((images[half:], first_half))
    others = [first_half, fetch(second_src)]
    slot_ids = jnp.arange(slots)
    plus = jnp.any((partners[0] == step + halo - 1) & (slot_ids < counts[0]))
    own_minus = jnp.any((partners[0] == halo - step) & (slot_ids < counts[0]))
    packed = jnp.concatenate([start[0], own_minus.astype(jnp.float32)[None]])
    other_packed = fetch(packed)
    minus = other_packed[width] > 0.5
    other_start = other_packed[:width]

    tile = pair_tile(images, others, table)

    col_bits = [1 << b for b in range(ncols.bit_length() - 1)]

    forward = jnp.where(plus, jnp.dot(tile, other_start, precision=HIGH), 0.0)
    backward = jnp.where(minus, jnp.dot(tile.T, start[0], precision=HIGH), 0.0)
    sent = jnp.concatenate([backward, tile.reshape(width * width), plus.astype(jnp.float32)[None]])
    got = lax.ppermute(sent, axes, back)
    y1 = butterfly_sum(forward + got[:width], axes, size, col_bits)
    tile_below = got[width : width + width * width].reshape(width, width)
    plus_below = got[width + width * width] > 0.5
    up = jnp.where(minus, jnp.dot(tile.T, y1, precision=HIGH), 0.0)
    down = jnp.where(plus_below, jnp.dot(tile_below, y1, precision=HIGH), 0.0)
    own_square = jnp.where(lax.axis_index("cols") == 0, jnp.sum(y1 * y1), 0.0)
    packet = jnp.concatenate([up, down, own_square[None]])
    gathered = lax.all_to_all(jnp.broadcast_to(packet, (size, 2 * width + 1)), axes, 0, 0, tiled=True)
    gathered = gathered.reshape(nblk, ncols, 2 * width + 1)
    ring = jnp.concatenate([gathered, gathered, gathered], axis=0)
    z_all = ring[nblk - 1 : 2 * nblk - 1, 0, :width]
    for c in range(1, ncols):
        z_all = z_all + ring[nblk - c - 1 : 2 * nblk - c - 1, c, :width]
    for c in range(ncols):
        z_all = z_all + ring[nblk + c + 1 : 2 * nblk + c + 1, c, width : 2 * width]
    sum_y1 = jnp.sum(gathered[:, :, 2 * width])
    sum_z = jnp.sum(z_all * z_all)
    z = lax.dynamic_index_in_dim(z_all, lax.axis_index("rows"), 0, keepdims=False)
    entries = float(width * nblk)
    s1 = jnp.sqrt(sum_y1 / entries + norm_eps)
    first_vec = y1 / s1
    second_raw = z / s1
    s2 = jnp.sqrt(sum_z / (s1 * s1) / entries + norm_eps)
    return (first_vec[None, :], (second_raw / s2)[None, :])


def solution(mesh):
    in_specs = (P("rows", None, None), P("rows", None), P("rows"), P("rows", None))
    out_specs = (P("rows", None), P("rows", None))
    return jax.shard_map(body, mesh=mesh, in_specs=in_specs, out_specs=out_specs, check_vma=False)
```

```python
import math

import jax
import jax.numpy as jnp
from jax import lax
from jax.experimental import pallas as pl
from jax.experimental.pallas import tpu as pltpu
from jax.sharding import PartitionSpec as P

score_gain = 0.4
norm_eps = 1e-06
HIGH = lax.Precision.HIGHEST
LOG2E = 1.4426950408889634


def line_table(lines):
    angle = 2.0 * math.pi * jnp.arange(lines).astype(jnp.float32) / lines
    return jnp.stack([jnp.cos(angle), jnp.sin(angle), jnp.cos(2.0 * angle)], axis=1)


def tile_kernel(a_ref, b_ref, w_ref, o_ref, s_ref):
    n = a_ref.shape[0]
    lines = w_ref.shape[1]
    nb = b_ref.shape[0] // lines
    width = a_ref.shape[1]
    groups = width // 128
    strips = lines // 8

    def per_image(a, carry):
        s_ref[...] = (
            lax.dot_general(
                b_ref[...], a_ref[a], (((1,), (1,)), ((), ())), preferred_element_type=jnp.float32
            )
            * (score_gain * LOG2E)
        )

        def per_partner(b, carry2):
            base = b * lines

            def col_max(r, m):
                start = pl.multiple_of(base + r * 8, 8)
                return jnp.maximum(m, s_ref[pl.ds(start, 8), :])

            m8 = lax.fori_loop(0, strips, col_max, jnp.full((8, width), -jnp.inf, jnp.float32), unroll=True)
            top = jnp.max(m8, axis=0, keepdims=True)
            top8 = jnp.broadcast_to(top, (8, width))

            def accumulate(r, acc):
                start = pl.multiple_of(base + r * 8, 8)
                e = jnp.exp2(s_ref[pl.ds(start, 8), :] - top8)
                row = pl.multiple_of(r * 8, 8)
                out = [acc[0] + e]
                for q in range(3):
                    wq = w_ref[q, pl.ds(row, 8), :]
                    wide = jnp.concatenate([wq] * groups, axis=1)
                    out.append(acc[q + 1] + e * wide)
                return tuple(out)

            zero = jnp.zeros((8, width), jnp.float32)
            acc = lax.fori_loop(0, strips, accumulate, (zero, zero, zero, zero), unroll=True)
            o_ref[a, b, 0:1, :] = top
            for j in range(4):
                o_ref[a, b, j + 1 : j + 2, :] = jnp.sum(acc[j], axis=0, keepdims=True)
            return carry2

        lax.fori_loop(0, nb, per_partner, 0)
        return carry

    lax.fori_loop(0, n, per_image, 0)


def pair_stats(own_p, other, wide):
    count, padded, radii = own_p.shape
    part, lines, _ = other.shape
    flops = 2 * count * part * lines * padded * radii + 12 * count * part * lines * padded
    return pl.pallas_call(
        tile_kernel,
        out_shape=jax.ShapeDtypeStruct((count, part, 8, padded), jnp.float32),
        in_specs=[pl.BlockSpec(memory_space=pltpu.VMEM)] * 3,
        out_specs=pl.BlockSpec(memory_space=pltpu.VMEM),
        scratch_shapes=[pltpu.VMEM((part * lines, padded), jnp.float32)],
        compiler_params=pltpu.CompilerParams(vmem_limit_bytes=48 * 1024 * 1024),
        cost_estimate=pl.CostEstimate(
            flops=flops, transcendentals=count * part * lines * padded, bytes_accessed=2 * 1024 * 1024
        ),
    )(own_p, other.reshape(part * lines, radii), wide)


def pair_tile(own, others, table):
    count, lines, radii = own.shape
    padded = ((lines + 127) // 128) * 128
    own_p = jnp.pad(own, ((0, 0), (0, padded - lines), (0, 0)))
    wide = jnp.broadcast_to(jnp.transpose(table)[:, :, None], (3, lines, 128))
    stats = jnp.concatenate([pair_stats(own_p, other, wide) for other in others], axis=1)
    stats = stats[:, :, :, :lines]
    top = stats[:, :, 0, :]
    peak = jnp.max(top, axis=2, keepdims=True)
    scale = jnp.exp2(top - peak)
    total = jnp.sum(scale * stats[:, :, 1, :], axis=2)
    sums = stats[:, :, 2:5, :] * scale[:, :, None, :]
    rel = jnp.sum(jnp.transpose(table)[None, None, :, None, :] * sums[:, :, None, :, :], axis=-1)
    rel = rel / total[:, :, None, None]
    return jnp.transpose(rel, (2, 0, 3, 1)).reshape(3 * count, 3 * count)


def butterfly_sum(value, axes, size, bits):
    for bit in bits:
        route = [(i, i ^ bit) for i in range(size)]
        value = value + lax.ppermute(value, axes, route)
    return value


def body(images, partners, counts, start):
    count, lines, radii = images.shape
    width = 3 * count
    slots = partners.shape[1]
    halo = slots // 2
    ncols = lax.axis_size("cols")
    nblk = lax.axis_size("rows")
    size = nblk * ncols
    step = lax.axis_index("cols") + 1
    table = line_table(lines)

    axes = ("rows", "cols")
    route = []
    for i in range(nblk):
        for c in range(ncols):
            route.append((((i + c + 1) % nblk) * ncols + c, i * ncols + c))
    back = [(dst, src) for src, dst in route]
    fetch = lambda v: lax.ppermute(v, axes, route)
    half = count // 2
    first_half = fetch(images[:half])
    second_src, first_half = lax.optimization_barrier((images[half:], first_half))
    others = [first_half, fetch(second_src)]
    slot_ids = jnp.arange(slots)
    plus = jnp.any((partners[0] == step + halo - 1) & (slot_ids < counts[0]))
    own_minus = jnp.any((partners[0] == halo - step) & (slot_ids < counts[0]))
    packed = jnp.concatenate([start[0], own_minus.astype(jnp.float32)[None]])
    other_packed = fetch(packed)
    minus = other_packed[width] > 0.5
    other_start = other_packed[:width]

    tile = pair_tile(images, others, table)

    col_bits = [1 << b for b in range(ncols.bit_length() - 1)]

    forward = jnp.where(plus, jnp.sum(tile * other_start[None, :], axis=1), 0.0)
    backward = jnp.where(minus, jnp.sum(tile * start[0][:, None], axis=0), 0.0)
    sent = jnp.concatenate([backward, tile.reshape(width * width), plus.astype(jnp.float32)[None]])
    got = lax.ppermute(sent, axes, back)
    y1 = butterfly_sum(forward + got[:width], axes, size, col_bits)
    tile_below = got[width : width + width * width].reshape(width, width)
    plus_below = got[width + width * width] > 0.5
    up = jnp.where(minus, jnp.sum(tile * y1[:, None], axis=0), 0.0)
    down = jnp.where(plus_below, jnp.sum(tile_below * y1[None, :], axis=1), 0.0)
    own_square = jnp.where(lax.axis_index("cols") == 0, jnp.sum(y1 * y1), 0.0)
    packet = jnp.concatenate([up, down, own_square[None]])
    gathered = lax.all_to_all(jnp.broadcast_to(packet, (size, 2 * width + 1)), axes, 0, 0, tiled=True)
    gathered = gathered.reshape(nblk, ncols, 2 * width + 1)
    ring = jnp.concatenate([gathered, gathered, gathered], axis=0)
    z_all = ring[nblk - 1 : 2 * nblk - 1, 0, :width]
    for c in range(1, ncols):
        z_all = z_all + ring[nblk - c - 1 : 2 * nblk - c - 1, c, :width]
    for c in range(ncols):
        z_all = z_all + ring[nblk + c + 1 : 2 * nblk + c + 1, c, width : 2 * width]
    sum_y1 = jnp.sum(gathered[:, :, 2 * width])
    sum_z = jnp.sum(z_all * z_all)
    z = lax.dynamic_index_in_dim(z_all, lax.axis_index("rows"), 0, keepdims=False)
    entries = float(width * nblk)
    s1 = jnp.sqrt(sum_y1 / entries + norm_eps)
    first_vec = y1 / s1
    second_raw = z / s1
    s2 = jnp.sqrt(sum_z / (s1 * s1) / entries + norm_eps)
    return (first_vec[None, :], (second_raw / s2)[None, :])


def solution(mesh):
    in_specs = (P("rows", None, None), P("rows", None), P("rows"), P("rows", None))
    out_specs = (P("rows", None), P("rows", None))
    return jax.shard_map(body, mesh=mesh, in_specs=in_specs, out_specs=out_specs, check_vma=False)
```

```python
import math

import jax
import jax.numpy as jnp
from jax import lax
from jax.experimental import pallas as pl
from jax.experimental.pallas import tpu as pltpu
from jax.sharding import PartitionSpec as P

score_gain = 0.4
norm_eps = 1e-06
HIGH = lax.Precision.HIGHEST
LOG2E = 1.4426950408889634


def line_table(lines):
    angle = 2.0 * math.pi * jnp.arange(lines).astype(jnp.float32) / lines
    return jnp.stack([jnp.cos(angle), jnp.sin(angle), jnp.cos(2.0 * angle)], axis=1)


def tile_kernel(a_ref, b_ref, w_ref, o_ref, s_ref):
    n = a_ref.shape[0]
    lines = w_ref.shape[1]
    nb = b_ref.shape[0] // lines
    width = a_ref.shape[1]
    groups = width // 128
    strips = lines // 8

    def per_image(a, carry):
        s_ref[...] = (
            lax.dot_general(
                b_ref[...], a_ref[a], (((1,), (1,)), ((), ())), preferred_element_type=jnp.float32
            )
            * (score_gain * LOG2E)
        )

        def per_partner(b, carry2):
            base = b * lines

            def col_max(r, m):
                start = pl.multiple_of(base + r * 8, 8)
                return jnp.maximum(m, s_ref[pl.ds(start, 8), :])

            m8 = lax.fori_loop(0, strips, col_max, jnp.full((8, width), -jnp.inf, jnp.float32), unroll=True)
            top = jnp.max(m8, axis=0, keepdims=True)
            top8 = jnp.broadcast_to(top, (8, width))

            def accumulate(r, acc):
                start = pl.multiple_of(base + r * 8, 8)
                e = jnp.exp2(s_ref[pl.ds(start, 8), :] - top8)
                row = pl.multiple_of(r * 8, 8)
                out = [acc[0] + e]
                for q in range(3):
                    wq = w_ref[q, pl.ds(row, 8), :]
                    wide = jnp.concatenate([wq] * groups, axis=1)
                    out.append(acc[q + 1] + e * wide)
                return tuple(out)

            zero = jnp.zeros((8, width), jnp.float32)
            acc = lax.fori_loop(0, strips, accumulate, (zero, zero, zero, zero), unroll=True)
            o_ref[a, b, 0:1, :] = top
            for j in range(4):
                o_ref[a, b, j + 1 : j + 2, :] = jnp.sum(acc[j], axis=0, keepdims=True)
            return carry2

        lax.fori_loop(0, nb, per_partner, 0)
        return carry

    lax.fori_loop(0, n, per_image, 0)


def pair_stats(own_p, other, wide):
    count, padded, radii = own_p.shape
    lines = wide.shape[1]
    part = other.shape[0] // lines
    flops = 2 * count * part * lines * padded * radii + 12 * count * part * lines * padded
    return pl.pallas_call(
        tile_kernel,
        out_shape=jax.ShapeDtypeStruct((count, part, 8, padded), jnp.float32),
        in_specs=[pl.BlockSpec(memory_space=pltpu.VMEM)] * 3,
        out_specs=pl.BlockSpec(memory_space=pltpu.VMEM),
        scratch_shapes=[pltpu.VMEM((part * lines, padded), jnp.float32)],
        compiler_params=pltpu.CompilerParams(vmem_limit_bytes=48 * 1024 * 1024),
        cost_estimate=pl.CostEstimate(
            flops=flops, transcendentals=count * part * lines * padded, bytes_accessed=2 * 1024 * 1024
        ),
    )(own_p, other, wide)


def pair_tile(own, others, table):
    count, lines, radii = own.shape
    padded = ((lines + 127) // 128) * 128
    own_p = jnp.pad(own, ((0, 0), (0, padded - lines), (0, 0)))
    wide = jnp.broadcast_to(jnp.transpose(table)[:, :, None], (3, lines, 128))
    stats = jnp.concatenate([pair_stats(own_p, other, wide) for other in others], axis=1)
    stats = stats[:, :, :, :lines]
    top = stats[:, :, 0, :]
    peak = jnp.max(top, axis=2, keepdims=True)
    scale = jnp.exp2(top - peak)
    total = jnp.sum(scale * stats[:, :, 1, :], axis=2)
    sums = stats[:, :, 2:5, :] * scale[:, :, None, :]
    rel = jnp.sum(jnp.transpose(table)[None, None, :, None, :] * sums[:, :, None, :, :], axis=-1)
    rel = rel / total[:, :, None, None]
    return jnp.transpose(rel, (2, 0, 3, 1)).reshape(3 * count, 3 * count)


def butterfly_sum(value, axes, size, bits):
    for bit in bits:
        route = [(i, i ^ bit) for i in range(size)]
        value = value + lax.ppermute(value, axes, route)
    return value


def body(images, partners, counts, start):
    count, lines, radii = images.shape
    width = 3 * count
    slots = partners.shape[1]
    halo = slots // 2
    ncols = lax.axis_size("cols")
    nblk = lax.axis_size("rows")
    size = nblk * ncols
    step = lax.axis_index("cols") + 1
    table = line_table(lines)

    axes = ("rows", "cols")
    route = []
    for i in range(nblk):
        for c in range(ncols):
            route.append((((i + c + 1) % nblk) * ncols + c, i * ncols + c))
    back = [(dst, src) for src, dst in route]
    fetch = lambda v: lax.ppermute(v, axes, route)
    half = count // 2
    first_half = fetch(images[:half].reshape(half * lines, radii))
    second_src, first_half = lax.optimization_barrier((images[half:].reshape((count - half) * lines, radii), first_half))
    others = [first_half, fetch(second_src)]
    slot_ids = jnp.arange(slots)
    plus = jnp.any((partners[0] == step + halo - 1) & (slot_ids < counts[0]))
    own_minus = jnp.any((partners[0] == halo - step) & (slot_ids < counts[0]))
    packed = jnp.concatenate([start[0], own_minus.astype(jnp.float32)[None]])
    other_packed = fetch(packed)
    minus = other_packed[width] > 0.5
    other_start = other_packed[:width]

    tile = pair_tile(images, others, table)

    col_bits = [1 << b for b in range(ncols.bit_length() - 1)]

    forward = jnp.where(plus, jnp.dot(tile, other_start, precision=HIGH), 0.0)
    backward = jnp.where(minus, jnp.dot(tile.T, start[0], precision=HIGH), 0.0)
    sent = jnp.concatenate([backward, tile.reshape(width * width), plus.astype(jnp.float32)[None]])
    got = lax.ppermute(sent, axes, back)
    y1 = butterfly_sum(forward + got[:width], axes, size, col_bits)
    tile_below = got[width : width + width * width].reshape(width, width)
    plus_below = got[width + width * width] > 0.5
    up = jnp.where(minus, jnp.dot(tile.T, y1, precision=HIGH), 0.0)
    down = jnp.where(plus_below, jnp.dot(tile_below, y1, precision=HIGH), 0.0)
    own_square = jnp.where(lax.axis_index("cols") == 0, jnp.sum(y1 * y1), 0.0)
    packet = jnp.concatenate([up, down, own_square[None]])
    gathered = lax.all_to_all(jnp.broadcast_to(packet, (size, 2 * width + 1)), axes, 0, 0, tiled=True)
    gathered = gathered.reshape(nblk, ncols, 2 * width + 1)
    ring = jnp.concatenate([gathered, gathered, gathered], axis=0)
    z_all = ring[nblk - 1 : 2 * nblk - 1, 0, :width]
    for c in range(1, ncols):
        z_all = z_all + ring[nblk - c - 1 : 2 * nblk - c - 1, c, :width]
    for c in range(ncols):
        z_all = z_all + ring[nblk + c + 1 : 2 * nblk + c + 1, c, width : 2 * width]
    sum_y1 = jnp.sum(gathered[:, :, 2 * width])
    sum_z = jnp.sum(z_all * z_all)
    z = lax.dynamic_index_in_dim(z_all, lax.axis_index("rows"), 0, keepdims=False)
    entries = float(width * nblk)
    s1 = jnp.sqrt(sum_y1 / entries + norm_eps)
    first_vec = y1 / s1
    second_raw = z / s1
    s2 = jnp.sqrt(sum_z / (s1 * s1) / entries + norm_eps)
    return (first_vec[None, :], (second_raw / s2)[None, :])


def solution(mesh):
    in_specs = (P("rows", None, None), P("rows", None), P("rows"), P("rows", None))
    out_specs = (P("rows", None), P("rows", None))
    return jax.shard_map(body, mesh=mesh, in_specs=in_specs, out_specs=out_specs, check_vma=False)
```
